256 devices in a mesh: dp: 32 (over x, z), segment: 2 (over core), rows: 4 (over y).
Axes of the slice: x: 4, y: 4, z: 8, core: 2. Of those that a mesh axis runs over, the one named last changes fastest.
Arguments:
- block_input: bfloat16 [32, 16, 32, 416], P('dp', 'rows'), may hold values from -6 to 6
- saved_maps: bfloat16 [2, 32, 16, 32, 2496], P('segment', 'dp', 'rows'), may hold values from -6 to 6
- grad_p5: bfloat16 [32, 16, 32, 384], P('dp', 'rows'), may hold values from -6 to 6
- grad_p6: bfloat16 [32, 8, 16, 384], P('dp', 'rows'), may hold values from -12 to 12
- grad_p7: bfloat16 [32, 4, 8, 384], P('dp', 'rows'), may hold values from -16 to 16
- lateral: bfloat16 [416, 384], replicated, may hold values from -0.3125 to 0.3125
- stacked: bfloat16 [2, 1038336], P('segment', ('dp', 'rows')), may hold values from -0.3125 to 0.3125
- kernel: bfloat16 [25, 2496], replicated, may hold values from -1.75 to 1.75
- se_reduce: bfloat16 [2496, 104], replicated, may hold values from -0.3125 to 0.3125
- se_expand: bfloat16 [104, 2496], replicated, may hold values from -1.25 to 1.25
Outputs:
- grad_inputs: bfloat16 [2, 32, 16, 32, 416], P('segment', 'dp', 'rows')
- param_grads: float32 [2, 1038336], P('segment', ('dp', 'rows'))
The draws below stay inside these ranges and needn't reach their ends.
All inputs are finite; a program needn't handle non-finite values.
Results may differ from the reference program's by a relative error of at most 0.0059.
Values may be sent and summed in bfloat16 or wider, within the bound.
No kernel may reach another device: no remote copies, remote signals or barrier semaphores. Data moves between devices by JAX's collectives and lax.ppermute only.
A program may use at most 64 MiB of HBM per device.

```python
import jax
import jax.numpy as jnp
from jax import lax

CIN = 416
LAT = 384
EXP = 2496
SER = 104
W = 32
BATCH = 32
H = 16


def block_levels(key, extent, cuts, low, high):
    level, own = 1.0, jax.random.fold_in(key, 6)
    for axis_at, blocks in cuts:
        draws = jnp.exp(jax.random.uniform(jax.random.fold_in(own, axis_at), (blocks,), jnp.float32, low / len(cuts), high / len(cuts)))
        level = level * jnp.repeat(draws, extent[axis_at] // blocks).reshape([-1 if axis == axis_at else 1 for axis in range(len(extent))])
    return level


def gaussian(rng, dims, spread, most, shards=(), kind=jnp.bfloat16):
    drawn = spread * jax.random.normal(rng, dims, jnp.float32)
    if shards:
        drawn = drawn * block_levels(rng, dims, shards, -0.22, 0.18)
    return jnp.clip(drawn, -most, most).astype(kind)


def setup_inputs(seed: int = 0) -> dict:
    key_of = jax.random.split(jax.random.key(seed), 11)
    return {
        "block_input": gaussian(key_of[0], (BATCH, H, W, CIN), 1.0, 6.0, ((0, 32), (1, 4))),
        "saved_maps": gaussian(key_of[1], (2, BATCH, H, W, EXP), 1.0, 6.0, ((0, 2), (1, 32), (2, 4))),
        "grad_p5": gaussian(key_of[2], (BATCH, H, W, LAT), 1.0, 6.0, ((0, 32), (1, 4))),
        "grad_p6": gaussian(key_of[3], (BATCH, H // 2, W // 2, LAT), 2.0, 12.0, ((0, 32), (1, 4))),
        "grad_p7": gaussian(key_of[4], (BATCH, H // 4, W // 4, LAT), 4.0, 16.0, ((0, 32), (1, 4))),
        "lateral": gaussian(key_of[5], (CIN, LAT), LAT ** -0.5, 0.3125),
        "stacked": gaussian(key_of[6], (2, CIN * EXP), CIN ** -0.5, 0.3125, ((0, 2), (1, 128))),
        "kernel": gaussian(key_of[7], (25, EXP), 12 ** -0.5, 1.75),
        "se_reduce": gaussian(key_of[8], (EXP, SER), (EXP // 8) ** -0.5, 0.3125),
        "se_expand": gaussian(key_of[9], (SER, EXP), (SER // 4) ** -0.5, 1.25),
    }


def up_two(v):
    return jnp.repeat(jnp.repeat(v, 2, axis=0), 2, axis=1)


def silu_slope(v):
    sig = jax.nn.sigmoid(v)
    return sig * (1.0 + v * (1.0 - sig))


def depth_forward(padded, taps, rows, cols):
    total = jnp.zeros((rows, cols, taps.shape[1]), jnp.float32)
    for p in range(5):
        for q in range(5):
            total = total + taps[5 * p + q] * padded[p:p + rows, q:q + cols].astype(jnp.float32)
    return total


def depth_backward(padded, taps, rows, cols):
    total = jnp.zeros((rows, cols, taps.shape[1]), jnp.float32)
    for p in range(5):
        for q in range(5):
            total = total + taps[5 * p + q] * padded[4 - p:4 - p + rows, 4 - q:4 - q + cols].astype(jnp.float32)
    return total


def reference(block_input, saved_maps, grad_p5, grad_p6, grad_p7, lateral, stacked, kernel, se_reduce, se_expand):
    proj = stacked[0].reshape(CIN, EXP)
    expand = stacked[1].reshape(CIN, EXP)
    taps = kernel.astype(jnp.float32)
    reduce_w = se_reduce.astype(jnp.float32)
    expand_w = se_expand.astype(jnp.float32)
    cells = H * W

    def one(carry, items):
        image, held, pre, g5, g6, g7 = items
        inner = g6.astype(jnp.float32) + up_two(g7.astype(jnp.float32)) / 4.0
        g = (g5.astype(jnp.float32) + up_two(inner) / 4.0).astype(jnp.bfloat16)
        grad_out = jnp.dot(g.reshape(cells, LAT), lateral.T, preferred_element_type=jnp.float32).astype(jnp.bfloat16)
        grad_proj = jnp.dot(grad_out, proj, preferred_element_type=jnp.float32).astype(jnp.bfloat16)
        term_p = jnp.dot(grad_out.T, held.reshape(cells, EXP), preferred_element_type=jnp.float32)
        pre32 = pre.astype(jnp.float32)
        expanded = jax.nn.silu(pre32).astype(jnp.bfloat16)
        padded = jnp.pad(expanded, ((2, 2), (2, 2), (0, 0)))
        dwo = depth_forward(padded, taps, H, W)
        act = jax.nn.silu(dwo)
        gp = grad_proj.reshape(H, W, EXP).astype(jnp.float32)
        pooled = jnp.sum(act, axis=(0, 1)) / cells
        dsum = jnp.sum(gp * act, axis=(0, 1))
        z1 = jnp.dot(pooled, reduce_w, precision=lax.Precision.HIGHEST)
        z2 = jnp.dot(jax.nn.silu(z1), expand_w, precision=lax.Precision.HIGHEST)
        gate = jax.nn.sigmoid(z2)
        dz2 = dsum * gate * (1.0 - gate)
        dz1 = jnp.dot(dz2, expand_w.T, precision=lax.Precision.HIGHEST) * silu_slope(z1)
        dpool = jnp.dot(dz1, reduce_w.T, precision=lax.Precision.HIGHEST)
        grad_dw = ((gp * gate + dpool / cells) * silu_slope(dwo)).astype(jnp.bfloat16)
        padded_grad = jnp.pad(grad_dw, ((2, 2), (2, 2), (0, 0)))
        grad_e = depth_backward(padded_grad, taps, H, W)
        grad_pre = (grad_e * silu_slope(pre32)).astype(jnp.bfloat16).reshape(cells, EXP)
        term_e = jnp.dot(image.reshape(cells, CIN).T, grad_pre, preferred_element_type=jnp.float32)
        grad_x = (grad_out.astype(jnp.float32) + jnp.dot(grad_pre, expand.T, preferred_element_type=jnp.float32)).astype(jnp.bfloat16)
        carry = (carry[0] + term_p, carry[1] + term_e)
        return carry, (grad_out.reshape(H, W, CIN), grad_x.reshape(H, W, CIN))

    start = (jnp.zeros((CIN, EXP), jnp.float32), jnp.zeros((CIN, EXP), jnp.float32))
    totals, outs = lax.scan(one, start, (block_input, saved_maps[0], saved_maps[1], grad_p5, grad_p6, grad_p7))
    grad_inputs = jnp.stack([outs[0], outs[1]], axis=0)
    param_grads = jnp.stack([totals[0].reshape(-1), totals[1].reshape(-1)], axis=0) / BATCH
    return grad_inputs, param_grads
```

```python
import jax
import jax.numpy as jnp
from jax import lax
from jax.sharding import PartitionSpec as P


def extended_2(block, sides, width):
    for axis, dim in sides:
        count = lax.axis_size(axis)
        forward = [(i, i + 1) for i in range(count - 1)]
        backward = [(target, source) for source, target in forward]
        low = lax.ppermute(
            lax.slice_in_dim(block, block.shape[dim] - width, None, axis=dim), axis, forward
        )
        high = lax.ppermute(lax.slice_in_dim(block, 0, width, axis=dim), axis, backward)
        block = jnp.concatenate([low, block, high], axis=dim)
    return block


def passed_along(array, axis, by):
    length = lax.axis_size(axis)
    pairs = [(i, i + by) for i in range(length) if 0 <= i + by < length]
    return lax.ppermute(array, axis, pairs)


def flat_bits():
    rows_bits = lax.axis_size("rows").bit_length() - 1
    dp_bits = lax.axis_size("dp").bit_length() - 1
    return [("rows", k) for k in range(rows_bits)] + [("dp", k) for k in range(dp_bits)]


def swap_pairs(axis, j):
    return [(i, i ^ (1 << j)) for i in range(lax.axis_size(axis))]


def gather_chunks(piece, order):
    bits = flat_bits()
    buf = piece
    lead = []
    for axis, j in order:
        recv = lax.ppermute(buf, axis, swap_pairs(axis, j))
        high = (lax.axis_index(axis) >> j) & 1
        buf = jnp.stack([jnp.where(high == 0, buf, recv), jnp.where(high == 0, recv, buf)])
        lead.insert(0, bits.index((axis, j)))
    count = len(bits)
    perm = [lead.index(k) for k in reversed(range(count))] + [count, count + 1]
    return jnp.transpose(buf, perm).reshape(-1)


def scatter_chunks(full, order):
    bits = flat_bits()
    count = len(bits)
    buf = full.reshape((2,) * count + full.shape[1:])
    live = list(reversed(range(count)))
    for axis, j in order:
        at = live.index(bits.index((axis, j)))
        high = (lax.axis_index(axis) >> j) & 1
        mine = lax.dynamic_index_in_dim(buf, high, at, keepdims=False)
        other = lax.dynamic_index_in_dim(buf, 1 - high, at, keepdims=False)
        buf = mine + lax.ppermute(other, axis, swap_pairs(axis, j))
        live.pop(at)
    return buf.reshape(-1)


def rows_sum(values):
    for j in range(lax.axis_size("rows").bit_length() - 1):
        values = tuple(v + lax.ppermute(v, "rows", swap_pairs("rows", j)) for v in values)
    return values


GATHER_ORDER = [("dp", 2), ("dp", 4), ("dp", 1), ("rows", 1), ("dp", 3), ("dp", 0), ("rows", 0)]
SCATTER_ORDER = GATHER_ORDER[::-1]


def up_two(v):
    return jnp.repeat(jnp.repeat(v, 2, axis=0), 2, axis=1)


def silu_slope(v):
    sig = jax.nn.sigmoid(v)
    return sig * (1.0 + v * (1.0 - sig))


def depth_forward(padded, taps, rows, cols):
    total = jnp.zeros((rows, cols, taps.shape[1]), jnp.float32)
    for p in range(5):
        for q in range(5):
            total = total + taps[5 * p + q] * padded[p : p + rows, q : q + cols].astype(jnp.float32)
    return total


def depth_backward(padded, taps, rows, cols):
    total = jnp.zeros((rows, cols, taps.shape[1]), jnp.float32)
    for p in range(5):
        for q in range(5):
            total = total + taps[5 * p + q] * padded[
                4 - p : 4 - p + rows, 4 - q : 4 - q + cols
            ].astype(jnp.float32)
    return total


def margin(values):
    extended = extended_2(values, (("rows", 0),), 2)
    return jnp.pad(extended, ((0, 0), (2, 2), (0, 0)))


def squeeze_gate(pool_total, grad_total, cells, reduce_w, expand_w):
    pooled = pool_total / cells
    z1 = jnp.dot(pooled, reduce_w, precision=lax.Precision.HIGHEST)
    z2 = jnp.dot(jax.nn.silu(z1), expand_w, precision=lax.Precision.HIGHEST)
    gate = jax.nn.sigmoid(z2)
    dz2 = grad_total * gate * (1.0 - gate)
    dz1 = jnp.dot(dz2, expand_w.T, precision=lax.Precision.HIGHEST) * silu_slope(z1)
    dpool = jnp.dot(dz1, reduce_w.T, precision=lax.Precision.HIGHEST)
    return (gate, dpool)


def body(
    block_input,
    saved_maps,
    grad_p5,
    grad_p6,
    grad_p7,
    lateral,
    stacked,
    kernel,
    se_reduce,
    se_expand,
):
    rows_here = block_input.shape[1]
    cols = block_input.shape[2]
    cin = block_input.shape[3]
    wide = saved_maps.shape[-1]
    cells_here = rows_here * cols
    row_count = lax.axis_size("rows")
    cells = cells_here * row_count
    images = block_input.shape[0] * lax.axis_size("dp")
    flat = gather_chunks(stacked[0].reshape(16, -1), GATHER_ORDER)
    weight = flat.reshape(cin, wide)
    segment = lax.axis_index("segment")
    held = saved_maps[0, 0]
    image = block_input[0]
    taps = kernel.astype(jnp.float32)
    reduce_w = se_reduce.astype(jnp.float32)
    expand_w = se_expand.astype(jnp.float32)

    def head_branch():
        inner = grad_p6[0].astype(jnp.float32) + up_two(grad_p7[0].astype(jnp.float32)) / 4.0
        g = (grad_p5[0].astype(jnp.float32) + up_two(inner) / 4.0).astype(jnp.bfloat16)
        grad_out = jnp.dot(
            g.reshape(cells_here, -1), lateral.T, preferred_element_type=jnp.float32
        ).astype(jnp.bfloat16)
        grad_proj = jnp.dot(grad_out, weight, preferred_element_type=jnp.float32).astype(
            jnp.bfloat16
        )
        term = jnp.dot(
            grad_out.T, held.reshape(cells_here, wide), preferred_element_type=jnp.float32
        )
        return (
            grad_out.reshape(rows_here, cols, cin),
            grad_proj.reshape(rows_here, cols, wide),
            term,
        )

    def rise_branch():
        expanded = jax.nn.silu(held.astype(jnp.float32)).astype(jnp.bfloat16)
        return (
            jnp.zeros((rows_here, cols, cin), jnp.bfloat16),
            expanded,
            jnp.zeros((cin, wide), jnp.float32),
        )

    grad_top, middle, head_term = lax.cond(segment == 0, head_branch, rise_branch)
    sent_top, sent_mid = passed_along((grad_top, middle), "segment", 1)
    padded_e = margin(middle)

    def pool_branch():
        dwo = depth_forward(padded_e, taps, rows_here, cols)
        act = jax.nn.silu(dwo)
        pool_part = jnp.sum(act, axis=(0, 1))
        grad_part = jnp.sum(sent_mid.astype(jnp.float32) * act, axis=(0, 1))
        return (dwo, pool_part, grad_part)

    def still_branch():
        return (
            jnp.zeros((rows_here, cols, wide), jnp.float32),
            jnp.zeros((wide,), jnp.float32),
            jnp.zeros((wide,), jnp.float32),
        )

    dwo, pool_part, grad_part = lax.cond(segment == 1, pool_branch, still_branch)
    pool_total, grad_total = rows_sum((pool_part, grad_part))

    def gate_branch():
        gate, dpool = squeeze_gate(pool_total, grad_total, cells, reduce_w, expand_w)
        return ((sent_mid.astype(jnp.float32) * gate + dpool / cells) * silu_slope(dwo)).astype(
            jnp.bfloat16
        )

    def quiet_branch():
        return jnp.zeros((rows_here, cols, wide), jnp.bfloat16)

    grad_dw = lax.cond(segment == 1, gate_branch, quiet_branch)
    padded_grad = margin(grad_dw)

    def tail_branch():
        grad_e = depth_backward(padded_grad, taps, rows_here, cols)
        grad_pre = (
            (grad_e * silu_slope(held.astype(jnp.float32)))
            .astype(jnp.bfloat16)
            .reshape(cells_here, wide)
        )
        term = jnp.dot(
            image.reshape(cells_here, cin).T, grad_pre, preferred_element_type=jnp.float32
        )
        back = jnp.dot(grad_pre, weight.T, preferred_element_type=jnp.float32)
        grad_x = (sent_top.reshape(cells_here, cin).astype(jnp.float32) + back).astype(jnp.bfloat16)
        return (grad_x.reshape(rows_here, cols, cin), term)

    def head_keep():
        return (grad_top, head_term)

    grad_here, term = lax.cond(segment == 1, tail_branch, head_keep)
    shards = lax.axis_size("dp") * row_count
    flat_term = (term / images).reshape(shards, 8, -1)
    share = scatter_chunks(flat_term, SCATTER_ORDER)
    return (grad_here[None, None], share[None])


def solution(mesh):
    in_specs = (
        P("dp", "rows", None, None),
        P("segment", "dp", "rows", None, None),
        P("dp", "rows", None, None),
        P("dp", "rows", None, None),
        P("dp", "rows", None, None),
        P(),
        P("segment", ("dp", "rows")),
        P(),
        P(),
        P(),
    )
    out_specs = (P("segment", "dp", "rows", None, None), P("segment", ("dp", "rows")))
    return jax.shard_map(body, mesh=mesh, in_specs=in_specs, out_specs=out_specs, check_vma=False)
```

```python
import jax
import jax.numpy as jnp
from jax import lax
from jax.sharding import PartitionSpec as P


def extended_2(block, sides, width):
    for axis, dim in sides:
        count = lax.axis_size(axis)
        forward = [(i, i + 1) for i in range(count - 1)]
        backward = [(target, source) for source, target in forward]
        low = lax.ppermute(
            lax.slice_in_dim(block, block.shape[dim] - width, None, axis=dim), axis, forward
        )
        high = lax.ppermute(lax.slice_in_dim(block, 0, width, axis=dim), axis, backward)
        block = jnp.concatenate([low, block, high], axis=dim)
    return block


def passed_along(array, axis, by):
    length = lax.axis_size(axis)
    pairs = [(i, i + by) for i in range(length) if 0 <= i + by < length]
    return lax.ppermute(array, axis, pairs)


def flat_bits():
    rows_bits = lax.axis_size("rows").bit_length() - 1
    dp_bits = lax.axis_size("dp").bit_length() - 1
    return [("rows", k) for k in range(rows_bits)] + [("dp", k) for k in range(dp_bits)]


def swap_pairs(axis, j):
    return [(i, i ^ (1 << j)) for i in range(lax.axis_size(axis))]


def gather_chunks(piece, order):
    bits = flat_bits()
    buf = piece
    lead = []
    for axis, j in order:
        recv = lax.ppermute(buf, axis, swap_pairs(axis, j))
        high = (lax.axis_index(axis) >> j) & 1
        buf = jnp.stack([jnp.where(high == 0, buf, recv), jnp.where(high == 0, recv, buf)])
        lead.insert(0, bits.index((axis, j)))
    count = len(bits)
    perm = [lead.index(k) for k in reversed(range(count))] + [count, count + 1]
    return jnp.transpose(buf, perm).reshape((2**count,) + piece.shape)


def gather_streams(piece, orders, cuts):
    parts = jnp.split(piece, cuts, axis=-1)
    done = [gather_chunks(part, order) for part, order in zip(parts, orders)]
    return jnp.concatenate(done, axis=-1).reshape(-1)


def scatter_chunks(full, order):
    bits = flat_bits()
    count = len(bits)
    buf = full.reshape((2,) * count + full.shape[1:])
    live = list(reversed(range(count)))
    for axis, j in order:
        at = live.index(bits.index((axis, j)))
        high = (lax.axis_index(axis) >> j) & 1
        mine = lax.dynamic_index_in_dim(buf, high, at, keepdims=False)
        other = lax.dynamic_index_in_dim(buf, 1 - high, at, keepdims=False)
        buf = mine + lax.ppermute(other, axis, swap_pairs(axis, j))
        live.pop(at)
    return buf


def scatter_streams(full, orders, cuts):
    parts = jnp.split(full, cuts, axis=-1)
    done = [scatter_chunks(part, order) for part, order in zip(parts, orders)]
    return jnp.concatenate(done, axis=-1).reshape(-1)


def rows_sum(values):
    for j in range(lax.axis_size("rows").bit_length() - 1):
        values = tuple(v + lax.ppermute(v, "rows", swap_pairs("rows", j)) for v in values)
    return values


GATHER_ORDERS = (
    [("dp", 2), ("dp", 4), ("dp", 1), ("rows", 1), ("dp", 3), ("dp", 0), ("rows", 0)],
    [("dp", 4), ("rows", 1), ("dp", 2), ("dp", 1), ("rows", 0), ("dp", 3), ("dp", 0)],
)
SCATTER_ORDERS = tuple(order[::-1] for order in GATHER_ORDERS)


def up_two(v):
    return jnp.repeat(jnp.repeat(v, 2, axis=0), 2, axis=1)


def silu_slope(v):
    sig = jax.nn.sigmoid(v)
    return sig * (1.0 + v * (1.0 - sig))


def depth_forward(padded, taps, rows, cols):
    total = jnp.zeros((rows, cols, taps.shape[1]), jnp.float32)
    for p in range(5):
        for q in range(5):
            total = total + taps[5 * p + q] * padded[p : p + rows, q : q + cols].astype(jnp.float32)
    return total


def depth_backward(padded, taps, rows, cols):
    total = jnp.zeros((rows, cols, taps.shape[1]), jnp.float32)
    for p in range(5):
        for q in range(5):
            total = total + taps[5 * p + q] * padded[
                4 - p : 4 - p + rows, 4 - q : 4 - q + cols
            ].astype(jnp.float32)
    return total


def margin(values):
    extended = extended_2(values, (("rows", 0),), 2)
    return jnp.pad(extended, ((0, 0), (2, 2), (0, 0)))


def squeeze_gate(pool_total, grad_total, cells, reduce_w, expand_w):
    pooled = pool_total / cells
    z1 = jnp.dot(pooled, reduce_w, precision=lax.Precision.HIGHEST)
    z2 = jnp.dot(jax.nn.silu(z1), expand_w, precision=lax.Precision.HIGHEST)
    gate = jax.nn.sigmoid(z2)
    dz2 = grad_total * gate * (1.0 - gate)
    dz1 = jnp.dot(dz2, expand_w.T, precision=lax.Precision.HIGHEST) * silu_slope(z1)
    dpool = jnp.dot(dz1, reduce_w.T, precision=lax.Precision.HIGHEST)
    return (gate, dpool)


def body(
    block_input,
    saved_maps,
    grad_p5,
    grad_p6,
    grad_p7,
    lateral,
    stacked,
    kernel,
    se_reduce,
    se_expand,
):
    rows_here = block_input.shape[1]
    cols = block_input.shape[2]
    cin = block_input.shape[3]
    wide = saved_maps.shape[-1]
    cells_here = rows_here * cols
    row_count = lax.axis_size("rows")
    cells = cells_here * row_count
    images = block_input.shape[0] * lax.axis_size("dp")
    flat = gather_streams(stacked[0].reshape(16, -1), GATHER_ORDERS, [254])
    weight = flat.reshape(cin, wide)
    segment = lax.axis_index("segment")
    held = saved_maps[0, 0]
    image = block_input[0]
    taps = kernel.astype(jnp.float32)
    reduce_w = se_reduce.astype(jnp.float32)
    expand_w = se_expand.astype(jnp.float32)

    def head_branch():
        inner = grad_p6[0].astype(jnp.float32) + up_two(grad_p7[0].astype(jnp.float32)) / 4.0
        g = (grad_p5[0].astype(jnp.float32) + up_two(inner) / 4.0).astype(jnp.bfloat16)
        grad_out = jnp.dot(
            g.reshape(cells_here, -1), lateral.T, preferred_element_type=jnp.float32
        ).astype(jnp.bfloat16)
        grad_proj = jnp.dot(grad_out, weight, preferred_element_type=jnp.float32).astype(
            jnp.bfloat16
        )
        term = jnp.dot(
            grad_out.T, held.reshape(cells_here, wide), preferred_element_type=jnp.float32
        )
        return (
            grad_out.reshape(rows_here, cols, cin),
            grad_proj.reshape(rows_here, cols, wide),
            term,
        )

    def rise_branch():
        expanded = jax.nn.silu(held.astype(jnp.float32)).astype(jnp.bfloat16)
        return (
            jnp.zeros((rows_here, cols, cin), jnp.bfloat16),
            expanded,
            jnp.zeros((cin, wide), jnp.float32),
        )

    grad_top, middle, head_term = lax.cond(segment == 0, head_branch, rise_branch)
    sent_top, sent_mid = passed_along((grad_top, middle), "segment", 1)
    padded_e = margin(middle)

    def pool_branch():
        dwo = depth_forward(padded_e, taps, rows_here, cols)
        act = jax.nn.silu(dwo)
        pool_part = jnp.sum(act, axis=(0, 1))
        grad_part = jnp.sum(sent_mid.astype(jnp.float32) * act, axis=(0, 1))
        return (dwo, pool_part, grad_part)

    def still_branch():
        return (
            jnp.zeros((rows_here, cols, wide), jnp.float32),
            jnp.zeros((wide,), jnp.float32),
            jnp.zeros((wide,), jnp.float32),
        )

    dwo, pool_part, grad_part = lax.cond(segment == 1, pool_branch, still_branch)
    pool_total, grad_total = rows_sum((pool_part, grad_part))

    def gate_branch():
        gate, dpool = squeeze_gate(pool_total, grad_total, cells, reduce_w, expand_w)
        return ((sent_mid.astype(jnp.float32) * gate + dpool / cells) * silu_slope(dwo)).astype(
            jnp.bfloat16
        )

    def quiet_branch():
        return jnp.zeros((rows_here, cols, wide), jnp.bfloat16)

    grad_dw = lax.cond(segment == 1, gate_branch, quiet_branch)
    padded_grad = margin(grad_dw)

    def tail_branch():
        grad_e = depth_backward(padded_grad, taps, rows_here, cols)
        grad_pre = (
            (grad_e * silu_slope(held.astype(jnp.float32)))
            .astype(jnp.bfloat16)
            .reshape(cells_here, wide)
        )
        term = jnp.dot(
            image.reshape(cells_here, cin).T, grad_pre, preferred_element_type=jnp.float32
        )
        back = jnp.dot(grad_pre, weight.T, preferred_element_type=jnp.float32)
        grad_x = (sent_top.reshape(cells_here, cin).astype(jnp.float32) + back).astype(jnp.bfloat16)
        return (grad_x.reshape(rows_here, cols, cin), term)

    def head_keep():
        return (grad_top, head_term)

    grad_here, term = lax.cond(segment == 1, tail_branch, head_keep)
    shards = lax.axis_size("dp") * row_count
    flat_term = (term / images).reshape(shards, 8, -1)
    share = scatter_streams(flat_term, SCATTER_ORDERS, [512])
    return (grad_here[None, None], share[None])


def solution(mesh):
    in_specs = (
        P("dp", "rows", None, None),
        P("segment", "dp", "rows", None, None),
        P("dp", "rows", None, None),
        P("dp", "rows", None, None),
        P("dp", "rows", None, None),
        P(),
        P("segment", ("dp", "rows")),
        P(),
        P(),
        P(),
    )
    out_specs = (P("segment", "dp", "rows", None, None), P("segment", ("dp", "rows")))
    return jax.shard_map(body, mesh=mesh, in_specs=in_specs, out_specs=out_specs, check_vma=False)
```

```python
import jax
import jax.numpy as jnp
from jax import lax
from jax.sharding import PartitionSpec as P


def extended_2(block, sides, width):
    for axis, dim in sides:
        count = lax.axis_size(axis)
        forward = [(i, i + 1) for i in range(count - 1)]
        backward = [(target, source) for source, target in forward]
        low = lax.ppermute(
            lax.slice_in_dim(block, block.shape[dim] - width, None, axis=dim), axis, forward
        )
        high = lax.ppermute(lax.slice_in_dim(block, 0, width, axis=dim), axis, backward)
        block = jnp.concatenate([low, block, high], axis=dim)
    return block


def passed_along(array, axis, by):
    length = lax.axis_size(axis)
    pairs = [(i, i + by) for i in range(length) if 0 <= i + by < length]
    return lax.ppermute(array, axis, pairs)


def flat_bits():
    rows_bits = lax.axis_size("rows").bit_length() - 1
    dp_bits = lax.axis_size("dp").bit_length() - 1
    return [("rows", k) for k in range(rows_bits)] + [("dp", k) for k in range(dp_bits)]


def swap_pairs(axis, j):
    return [(i, i ^ (1 << j)) for i in range(lax.axis_size(axis))]


def gather_chunks(piece, order):
    bits = flat_bits()
    buf = piece
    lead = []
    for axis, j in order:
        recv = lax.ppermute(buf, axis, swap_pairs(axis, j))
        high = (lax.axis_index(axis) >> j) & 1
        buf = jnp.stack([jnp.where(high == 0, buf, recv), jnp.where(high == 0, recv, buf)])
        lead.insert(0, bits.index((axis, j)))
    count = len(bits)
    perm = [lead.index(k) for k in reversed(range(count))] + [count, count + 1]
    return jnp.transpose(buf, perm).reshape((2**count,) + piece.shape)


def gather_streams(piece, orders, cuts):
    parts = jnp.split(piece, cuts, axis=-1)
    done = [gather_chunks(part, order) for part, order in zip(parts, orders)]
    return jnp.concatenate(done, axis=-1).reshape(-1)


def scatter_chunks(full, order):
    bits = flat_bits()
    count = len(bits)
    buf = full.reshape((2,) * count + full.shape[1:])
    live = list(reversed(range(count)))
    for axis, j in order:
        at = live.index(bits.index((axis, j)))
        high = (lax.axis_index(axis) >> j) & 1
        mine = lax.dynamic_index_in_dim(buf, high, at, keepdims=False)
        other = lax.dynamic_index_in_dim(buf, 1 - high, at, keepdims=False)
        buf = mine + lax.ppermute(other, axis, swap_pairs(axis, j))
        live.pop(at)
    return buf


def scatter_streams(full, orders, cuts):
    parts = jnp.split(full, cuts, axis=-1)
    done = [scatter_chunks(part, order) for part, order in zip(parts, orders)]
    return jnp.concatenate(done, axis=-1).reshape(-1)


def rows_sum(values):
    for j in range(lax.axis_size("rows").bit_length() - 1):
        values = tuple(v + lax.ppermute(v, "rows", swap_pairs("rows", j)) for v in values)
    return values


GATHER_ORDERS = (
    [("dp", 2), ("dp", 4), ("dp", 1), ("rows", 1), ("dp", 3), ("dp", 0), ("rows", 0)],
    [("dp", 4), ("rows", 1), ("dp", 2), ("dp", 1), ("rows", 0), ("dp", 3), ("dp", 0)],
)
SCATTER_ORDERS = tuple(order[::-1] for order in GATHER_ORDERS)


def up_two(v):
    return jnp.repeat(jnp.repeat(v, 2, axis=0), 2, axis=1)


def silu_slope(v):
    sig = jax.nn.sigmoid(v)
    return sig * (1.0 + v * (1.0 - sig))


def depth_forward(padded, taps, rows, cols):
    total = jnp.zeros((rows, cols, taps.shape[1]), jnp.float32)
    for p in range(5):
        for q in range(5):
            total = total + taps[5 * p + q] * padded[p : p + rows, q : q + cols].astype(jnp.float32)
    return total


def depth_backward(padded, taps, rows, cols):
    total = jnp.zeros((rows, cols, taps.shape[1]), jnp.float32)
    for p in range(5):
        for q in range(5):
            total = total + taps[5 * p + q] * padded[
                4 - p : 4 - p + rows, 4 - q : 4 - q + cols
            ].astype(jnp.float32)
    return total


def margin(values):
    extended = extended_2(values, (("rows", 0),), 2)
    return jnp.pad(extended, ((0, 0), (2, 2), (0, 0)))


def squeeze_gate(pool_total, grad_total, cells, reduce_w, expand_w):
    pooled = pool_total / cells
    z1 = jnp.dot(pooled, reduce_w, precision=lax.Precision.HIGHEST)
    z2 = jnp.dot(jax.nn.silu(z1), expand_w, precision=lax.Precision.HIGHEST)
    gate = jax.nn.sigmoid(z2)
    dz2 = grad_total * gate * (1.0 - gate)
    dz1 = jnp.dot(dz2, expand_w.T, precision=lax.Precision.HIGHEST) * silu_slope(z1)
    dpool = jnp.dot(dz1, reduce_w.T, precision=lax.Precision.HIGHEST)
    return (gate, dpool)


def body(
    block_input,
    saved_maps,
    grad_p5,
    grad_p6,
    grad_p7,
    lateral,
    stacked,
    kernel,
    se_reduce,
    se_expand,
):
    rows_here = block_input.shape[1]
    cols = block_input.shape[2]
    cin = block_input.shape[3]
    wide = saved_maps.shape[-1]
    cells_here = rows_here * cols
    row_count = lax.axis_size("rows")
    cells = cells_here * row_count
    images = block_input.shape[0] * lax.axis_size("dp")
    flat = gather_streams(stacked[0].reshape(16, -1), GATHER_ORDERS, [254])
    weight = flat.reshape(cin, wide)
    segment = lax.axis_index("segment")
    held = saved_maps[0, 0]
    image = block_input[0]
    taps = kernel.astype(jnp.float32)
    reduce_w = se_reduce.astype(jnp.float32)
    expand_w = se_expand.astype(jnp.float32)

    def rise_branch():
        return jax.nn.silu(held.astype(jnp.float32)).astype(jnp.bfloat16)

    def rise_still():
        return jnp.zeros((rows_here, cols, wide), jnp.bfloat16)

    expanded = lax.cond(segment == 1, rise_branch, rise_still)
    padded_e = margin(expanded)

    def pool_branch():
        dwo = depth_forward(padded_e, taps, rows_here, cols)
        act = jax.nn.silu(dwo)
        return (dwo, act, jnp.sum(act, axis=(0, 1)))

    def still_branch():
        return (
            jnp.zeros((rows_here, cols, wide), jnp.float32),
            jnp.zeros((rows_here, cols, wide), jnp.float32),
            jnp.zeros((wide,), jnp.float32),
        )

    dwo, act, pool_part = lax.cond(segment == 1, pool_branch, still_branch)

    def head_branch():
        inner = grad_p6[0].astype(jnp.float32) + up_two(grad_p7[0].astype(jnp.float32)) / 4.0
        g = (grad_p5[0].astype(jnp.float32) + up_two(inner) / 4.0).astype(jnp.bfloat16)
        grad_out = jnp.dot(
            g.reshape(cells_here, -1), lateral.T, preferred_element_type=jnp.float32
        ).astype(jnp.bfloat16)
        grad_proj = jnp.dot(grad_out, weight, preferred_element_type=jnp.float32).astype(
            jnp.bfloat16
        )
        term = jnp.dot(
            grad_out.T, held.reshape(cells_here, wide), preferred_element_type=jnp.float32
        )
        return (
            grad_out.reshape(rows_here, cols, cin),
            grad_proj.reshape(rows_here, cols, wide),
            term,
        )

    def head_still():
        return (
            jnp.zeros((rows_here, cols, cin), jnp.bfloat16),
            jnp.zeros((rows_here, cols, wide), jnp.bfloat16),
            jnp.zeros((cin, wide), jnp.float32),
        )

    grad_top, grad_proj, head_term = lax.cond(segment == 0, head_branch, head_still)
    shards = lax.axis_size("dp") * row_count
    chunk = cin * wide // shards

    def spread(term):
        flat_term = (term / images).reshape(shards, 8, -1)
        return scatter_streams(flat_term, SCATTER_ORDERS, [512])

    def spread_still(term):
        return jnp.zeros((chunk,), jnp.float32)

    head_share = lax.cond(segment == 0, spread, spread_still, head_term)
    sent_top, sent_mid = passed_along((grad_top, grad_proj), "segment", 1)
    grad_part = jnp.sum(sent_mid.astype(jnp.float32) * act, axis=(0, 1))
    pool_total, grad_total = rows_sum((pool_part, grad_part))

    def gate_branch():
        gate, dpool = squeeze_gate(pool_total, grad_total, cells, reduce_w, expand_w)
        return ((sent_mid.astype(jnp.float32) * gate + dpool / cells) * silu_slope(dwo)).astype(
            jnp.bfloat16
        )

    def quiet_branch():
        return jnp.zeros((rows_here, cols, wide), jnp.bfloat16)

    grad_dw = lax.cond(segment == 1, gate_branch, quiet_branch)
    padded_grad = margin(grad_dw)

    def tail_branch():
        grad_e = depth_backward(padded_grad, taps, rows_here, cols)
        grad_pre = (
            (grad_e * silu_slope(held.astype(jnp.float32)))
            .astype(jnp.bfloat16)
            .reshape(cells_here, wide)
        )
        term = jnp.dot(
            image.reshape(cells_here, cin).T, grad_pre, preferred_element_type=jnp.float32
        )
        back = jnp.dot(grad_pre, weight.T, preferred_element_type=jnp.float32)
        grad_x = (sent_top.reshape(cells_here, cin).astype(jnp.float32) + back).astype(jnp.bfloat16)
        return (grad_x.reshape(rows_here, cols, cin), spread(term))

    def head_keep():
        return (grad_top, head_share)

    grad_here, share = lax.cond(segment == 1, tail_branch, head_keep)
    return (grad_here[None, None], share[None])


def solution(mesh):
    in_specs = (
        P("dp", "rows", None, None),
        P("segment", "dp", "rows", None, None),
        P("dp", "rows", None, None),
        P("dp", "rows", None, None),
        P("dp", "rows", None, None),
        P(),
        P("segment", ("dp", "rows")),
        P(),
        P(),
        P(),
    )
    out_specs = (P("segment", "dp", "rows", None, None), P("segment", ("dp", "rows")))
    return jax.shard_map(body, mesh=mesh, in_specs=in_specs, out_specs=out_specs, check_vma=False)
```

```python
import jax
import jax.numpy as jnp
from jax import lax
from jax.sharding import PartitionSpec as P


def extended_2(block, sides, width):
    for axis, dim in sides:
        count = lax.axis_size(axis)
        forward = [(i, i + 1) for i in range(count - 1)]
        backward = [(target, source) for source, target in forward]
        low = lax.ppermute(
            lax.slice_in_dim(block, block.shape[dim] - width, None, axis=dim), axis, forward
        )
        high = lax.ppermute(lax.slice_in_dim(block, 0, width, axis=dim), axis, backward)
        block = jnp.concatenate([low, block, high], axis=dim)
    return block


def passed_along(array, axis, by):
    length = lax.axis_size(axis)
    pairs = [(i, i + by) for i in range(length) if 0 <= i + by < length]
    return lax.ppermute(array, axis, pairs)


def flat_bits():
    rows_bits = lax.axis_size("rows").bit_length() - 1
    dp_bits = lax.axis_size("dp").bit_length() - 1
    return [("rows", k) for k in range(rows_bits)] + [("dp", k) for k in range(dp_bits)]


def swap_pairs(axis, j):
    return [(i, i ^ (1 << j)) for i in range(lax.axis_size(axis))]


def gather_chunks(piece, order):
    bits = flat_bits()
    buf = piece
    lead = []
    for axis, j in order:
        recv = lax.ppermute(buf, axis, swap_pairs(axis, j))
        high = (lax.axis_index(axis) >> j) & 1
        buf = jnp.stack([jnp.where(high == 0, buf, recv), jnp.where(high == 0, recv, buf)])
        lead.insert(0, bits.index((axis, j)))
    count = len(bits)
    perm = [lead.index(k) for k in reversed(range(count))] + [count, count + 1]
    return jnp.transpose(buf, perm).reshape((2**count,) + piece.shape)


def gather_streams(piece, orders, cuts):
    parts = jnp.split(piece, cuts, axis=-1)
    done = [gather_chunks(part, order) for part, order in zip(parts, orders)]
    return jnp.concatenate(done, axis=-1).reshape(-1)


def scatter_chunks(full, order):
    bits = flat_bits()
    count = len(bits)
    buf = full.reshape((2,) * count + full.shape[1:])
    live = list(reversed(range(count)))
    for axis, j in order:
        at = live.index(bits.index((axis, j)))
        high = (lax.axis_index(axis) >> j) & 1
        mine = lax.dynamic_index_in_dim(buf, high, at, keepdims=False)
        other = lax.dynamic_index_in_dim(buf, 1 - high, at, keepdims=False)
        buf = mine + lax.ppermute(other, axis, swap_pairs(axis, j))
        live.pop(at)
    return buf


def scatter_streams(full, orders, cuts):
    parts = jnp.split(full, cuts, axis=-1)
    done = [scatter_chunks(part, order) for part, order in zip(parts, orders)]
    return jnp.concatenate(done, axis=-1).reshape(-1)


def rows_sum(values):
    for j in range(lax.axis_size("rows").bit_length() - 1):
        values = tuple(v + lax.ppermute(v, "rows", swap_pairs("rows", j)) for v in values)
    return values


GATHER_ORDERS = (
    [("dp", 2), ("dp", 4), ("dp", 1), ("rows", 1), ("dp", 3), ("dp", 0), ("rows", 0)],
    [("dp", 4), ("rows", 1), ("dp", 2), ("dp", 1), ("rows", 0), ("dp", 3), ("dp", 0)],
)
SCATTER_ORDERS = tuple(order[::-1] for order in GATHER_ORDERS)


def up_two(v):
    return jnp.repeat(jnp.repeat(v, 2, axis=0), 2, axis=1)


def silu_slope(v):
    sig = jax.nn.sigmoid(v)
    return sig * (1.0 + v * (1.0 - sig))


def depth_forward(padded, taps, rows, cols):
    total = jnp.zeros((rows, cols, taps.shape[1]), jnp.float32)
    for p in range(5):
        for q in range(5):
            total = total + taps[5 * p + q] * padded[p : p + rows, q : q + cols].astype(jnp.float32)
    return total


def depth_backward(padded, taps, rows, cols):
    total = jnp.zeros((rows, cols, taps.shape[1]), jnp.float32)
    for p in range(5):
        for q in range(5):
            total = total + taps[5 * p + q] * padded[
                4 - p : 4 - p + rows, 4 - q : 4 - q + cols
            ].astype(jnp.float32)
    return total


def margin(values):
    extended = extended_2(values, (("rows", 0),), 2)
    return jnp.pad(extended, ((0, 0), (2, 2), (0, 0)))


def squeeze_gate(pool_total, grad_total, cells, reduce_w, expand_w):
    pooled = pool_total / cells
    z1 = jnp.dot(pooled, reduce_w, precision=lax.Precision.HIGHEST)
    z2 = jnp.dot(jax.nn.silu(z1), expand_w, precision=lax.Precision.HIGHEST)
    gate = jax.nn.sigmoid(z2)
    dz2 = grad_total * gate * (1.0 - gate)
    dz1 = jnp.dot(dz2, expand_w.T, precision=lax.Precision.HIGHEST) * silu_slope(z1)
    dpool = jnp.dot(dz1, reduce_w.T, precision=lax.Precision.HIGHEST)
    return (gate, dpool)


def body(
    block_input,
    saved_maps,
    grad_p5,
    grad_p6,
    grad_p7,
    lateral,
    stacked,
    kernel,
    se_reduce,
    se_expand,
):
    rows_here = block_input.shape[1]
    cols = block_input.shape[2]
    cin = block_input.shape[3]
    wide = saved_maps.shape[-1]
    cells_here = rows_here * cols
    row_count = lax.axis_size("rows")
    cells = cells_here * row_count
    images = block_input.shape[0] * lax.axis_size("dp")
    flat = gather_streams(stacked[0].reshape(16, -1), GATHER_ORDERS, [254])
    weight = flat.reshape(cin, wide)
    segment = lax.axis_index("segment")
    held = saved_maps[0, 0]
    image = block_input[0]
    taps = kernel.astype(jnp.float32)
    reduce_w = se_reduce.astype(jnp.float32)
    expand_w = se_expand.astype(jnp.float32)

    def rise_branch():
        return jax.nn.silu(held.astype(jnp.float32)).astype(jnp.bfloat16)

    def rise_still():
        return jnp.zeros((rows_here, cols, wide), jnp.bfloat16)

    expanded = lax.cond(segment == 1, rise_branch, rise_still)
    padded_e = margin(expanded)

    def pool_branch():
        dwo = depth_forward(padded_e, taps, rows_here, cols)
        act = jax.nn.silu(dwo)
        return (dwo, act, jnp.sum(act, axis=(0, 1)))

    def still_branch():
        return (
            jnp.zeros((rows_here, cols, wide), jnp.float32),
            jnp.zeros((rows_here, cols, wide), jnp.float32),
            jnp.zeros((wide,), jnp.float32),
        )

    dwo, act, pool_part = lax.cond(segment == 1, pool_branch, still_branch)

    def head_branch():
        inner = grad_p6[0].astype(jnp.float32) + up_two(grad_p7[0].astype(jnp.float32)) / 4.0
        g = (grad_p5[0].astype(jnp.float32) + up_two(inner) / 4.0).astype(jnp.bfloat16)
        grad_out = jnp.dot(
            g.reshape(cells_here, -1), lateral.T, preferred_element_type=jnp.float32
        ).astype(jnp.bfloat16)
        grad_proj = jnp.dot(grad_out, weight, preferred_element_type=jnp.float32).astype(
            jnp.bfloat16
        )
        term = jnp.dot(
            grad_out.T, held.reshape(cells_here, wide), preferred_element_type=jnp.float32
        )
        return (
            grad_out.reshape(rows_here, cols, cin),
            grad_proj.reshape(rows_here, cols, wide),
            term,
        )

    def head_still():
        return (
            jnp.zeros((rows_here, cols, cin), jnp.bfloat16),
            jnp.zeros((rows_here, cols, wide), jnp.bfloat16),
            jnp.zeros((cin, wide), jnp.float32),
        )

    grad_top, grad_proj, head_term = lax.cond(segment == 0, head_branch, head_still)
    shards = lax.axis_size("dp") * row_count
    chunk = cin * wide // shards

    def spread(term):
        flat_term = (term / images).reshape(shards, 8, -1)
        return scatter_streams(flat_term, SCATTER_ORDERS, [512])

    def spread_still(term):
        return jnp.zeros((chunk,), jnp.float32)

    sent_top, sent_mid = passed_along((grad_top, grad_proj), "segment", 1)
    sent_top, sent_mid, head_term = lax.optimization_barrier((sent_top, sent_mid, head_term))
    head_share = lax.cond(segment == 0, spread, spread_still, head_term)
    head_share, sent_top, sent_mid, act = lax.optimization_barrier(
        (head_share, sent_top, sent_mid, act)
    )
    grad_part = jnp.sum(sent_mid.astype(jnp.float32) * act, axis=(0, 1))
    pool_total, grad_total = rows_sum((pool_part, grad_part))

    def gate_branch():
        gate, dpool = squeeze_gate(pool_total, grad_total, cells, reduce_w, expand_w)
        return ((sent_mid.astype(jnp.float32) * gate + dpool / cells) * silu_slope(dwo)).astype(
            jnp.bfloat16
        )

    def quiet_branch():
        return jnp.zeros((rows_here, cols, wide), jnp.bfloat16)

    grad_dw = lax.cond(segment == 1, gate_branch, quiet_branch)
    padded_grad = margin(grad_dw)

    def tail_branch():
        grad_e = depth_backward(padded_grad, taps, rows_here, cols)
        grad_pre = (
            (grad_e * silu_slope(held.astype(jnp.float32)))
            .astype(jnp.bfloat16)
            .reshape(cells_here, wide)
        )
        term = jnp.dot(
            image.reshape(cells_here, cin).T, grad_pre, preferred_element_type=jnp.float32
        )
        back = jnp.dot(grad_pre, weight.T, preferred_element_type=jnp.float32)
        grad_x = (sent_top.reshape(cells_here, cin).astype(jnp.float32) + back).astype(jnp.bfloat16)
        return (grad_x.reshape(rows_here, cols, cin), spread(term))

    def head_keep():
        return (grad_top, head_share)

    grad_here, share = lax.cond(segment == 1, tail_branch, head_keep)
    return (grad_here[None, None], share[None])


def solution(mesh):
    in_specs = (
        P("dp", "rows", None, None),
        P("segment", "dp", "rows", None, None),
        P("dp", "rows", None, None),
        P("dp", "rows", None, None),
        P("dp", "rows", None, None),
        P(),
        P("segment", ("dp", "rows")),
        P(),
        P(),
        P(),
    )
    out_specs = (P("segment", "dp", "rows", None, None), P("segment", ("dp", "rows")))
    return jax.shard_map(body, mesh=mesh, in_specs=in_specs, out_specs=out_specs, check_vma=False)
```

```python
import jax
import jax.numpy as jnp
from jax import lax
from jax.sharding import PartitionSpec as P


def extended_2(block, sides, width):
    for axis, dim in sides:
        count = lax.axis_size(axis)
        forward = [(i, i + 1) for i in range(count - 1)]
        backward = [(target, source) for source, target in forward]
        low = lax.ppermute(
            lax.slice_in_dim(block, block.shape[dim] - width, None, axis=dim), axis, forward
        )
        high = lax.ppermute(lax.slice_in_dim(block, 0, width, axis=dim), axis, backward)
        block = jnp.concatenate([low, block, high], axis=dim)
    return block


def passed_along(array, axis, by):
    length = lax.axis_size(axis)
    pairs = [(i, i + by) for i in range(length) if 0 <= i + by < length]
    return lax.ppermute(array, axis, pairs)


def flat_bits():
    rows_bits = lax.axis_size("rows").bit_length() - 1
    dp_bits = lax.axis_size("dp").bit_length() - 1
    return [("rows", k) for k in range(rows_bits)] + [("dp", k) for k in range(dp_bits)]


def swap_pairs(axis, j):
    return [(i, i ^ (1 << j)) for i in range(lax.axis_size(axis))]


def gather_chunks(piece, order):
    bits = flat_bits()
    buf = piece
    lead = []
    for axis, j in order:
        recv = lax.ppermute(buf, axis, swap_pairs(axis, j))
        high = (lax.axis_index(axis) >> j) & 1
        buf = jnp.stack([jnp.where(high == 0, buf, recv), jnp.where(high == 0, recv, buf)])
        lead.insert(0, bits.index((axis, j)))
    count = len(bits)
    perm = [lead.index(k) for k in reversed(range(count))] + [count, count + 1]
    return jnp.transpose(buf, perm).reshape((2**count,) + piece.shape)


def gather_streams(piece, orders, cuts):
    parts = jnp.split(piece, cuts, axis=-1)
    done = [gather_rounds(part, order) for part, order in zip(parts, orders)]
    return jnp.concatenate(done, axis=-1).reshape(-1)


def scatter_chunks(full, order):
    bits = flat_bits()
    count = len(bits)
    buf = full.reshape((2,) * count + full.shape[1:])
    live = list(reversed(range(count)))
    for axis, j in order:
        at = live.index(bits.index((axis, j)))
        high = (lax.axis_index(axis) >> j) & 1
        mine = lax.dynamic_index_in_dim(buf, high, at, keepdims=False)
        other = lax.dynamic_index_in_dim(buf, 1 - high, at, keepdims=False)
        buf = mine + lax.ppermute(other, axis, swap_pairs(axis, j))
        live.pop(at)
    return buf


def scatter_streams(full, orders, cuts):
    parts = jnp.split(full, cuts, axis=-1)
    done = [scatter_rounds(part, order) for part, order in zip(parts, orders)]
    return jnp.concatenate(done, axis=-1).reshape(-1)


def rows_sum(values):
    for j in range(lax.axis_size("rows").bit_length() - 1):
        values = tuple(v + lax.ppermute(v, "rows", swap_pairs("rows", j)) for v in values)
    return values


GATHER_ORDERS = (
    [("dp", 2), ("dp", 4), ("dp", 1), ("rows", 1), ("dp", 3), ("dp", 0), ("rows", 0)],
    [("dp", 4), ("rows", 1), ("dp", 2), ("dp", 1), ("rows", 0), ("dp", 3), ("dp", 0)],
)
SCATTER_ORDERS = tuple(order[::-1] for order in GATHER_ORDERS)


GROUPS = {"x": ("dp", 3, 2), "z": ("dp", 0, 3), "y": ("rows", 0, 2)}
NATURAL = ("x", "z", "y")


def group_digit(group):
    axis, low, width = GROUPS[group]
    return (lax.axis_index(axis) >> low) & ((1 << width) - 1)


def shift_pairs(group, step):
    axis, low, width = GROUPS[group]
    count = 1 << width
    pairs = []
    for i in range(lax.axis_size(axis)):
        digit = (i >> low) & (count - 1)
        pairs.append((i, i - (digit << low) + (((digit + step) % count) << low)))
    return pairs


def gather_rounds(piece, order):
    buf = piece
    lead = []
    for group in order:
        count = 1 << GROUPS[group][2]
        got = [buf] + [
            lax.ppermute(buf, GROUPS[group][0], shift_pairs(group, -step))
            for step in range(1, count)
        ]
        buf = jnp.roll(jnp.stack(got), group_digit(group), axis=0)
        lead.insert(0, group)
    perm = [lead.index(group) for group in NATURAL]
    perm += list(range(len(NATURAL), buf.ndim))
    return jnp.transpose(buf, perm).reshape((-1,) + piece.shape)


def scatter_rounds(full, order):
    sizes = tuple(1 << GROUPS[group][2] for group in NATURAL)
    buf = full.reshape(sizes + full.shape[1:])
    live = list(NATURAL)
    for group in order:
        count = 1 << GROUPS[group][2]
        at = live.index(group)
        mine = group_digit(group)
        total = lax.dynamic_index_in_dim(buf, mine, at, keepdims=False)
        for step in range(1, count):
            piece = lax.dynamic_index_in_dim(buf, (mine + step) % count, at, keepdims=False)
            total = total + lax.ppermute(piece, GROUPS[group][0], shift_pairs(group, step))
        buf = total
        live.pop(at)
    return buf


GATHER_ROUNDS = (("z", "y", "x"), ("z", "x", "y"))
SCATTER_ROUNDS = tuple(order[::-1] for order in GATHER_ROUNDS)


def up_two(v):
    return jnp.repeat(jnp.repeat(v, 2, axis=0), 2, axis=1)


def silu_slope(v):
    sig = jax.nn.sigmoid(v)
    return sig * (1.0 + v * (1.0 - sig))


def depth_forward(padded, taps, rows, cols):
    total = jnp.zeros((rows, cols, taps.shape[1]), jnp.float32)
    for p in range(5):
        for q in range(5):
            total = total + taps[5 * p + q] * padded[p : p + rows, q : q + cols].astype(jnp.float32)
    return total


def depth_backward(padded, taps, rows, cols):
    total = jnp.zeros((rows, cols, taps.shape[1]), jnp.float32)
    for p in range(5):
        for q in range(5):
            total = total + taps[5 * p + q] * padded[
                4 - p : 4 - p + rows, 4 - q : 4 - q + cols
            ].astype(jnp.float32)
    return total


def margin(values):
    extended = extended_2(values, (("rows", 0),), 2)
    return jnp.pad(extended, ((0, 0), (2, 2), (0, 0)))


def squeeze_gate(pool_total, grad_total, cells, reduce_w, expand_w):
    pooled = pool_total / cells
    z1 = jnp.dot(pooled, reduce_w, precision=lax.Precision.HIGHEST)
    z2 = jnp.dot(jax.nn.silu(z1), expand_w, precision=lax.Precision.HIGHEST)
    gate = jax.nn.sigmoid(z2)
    dz2 = grad_total * gate * (1.0 - gate)
    dz1 = jnp.dot(dz2, expand_w.T, precision=lax.Precision.HIGHEST) * silu_slope(z1)
    dpool = jnp.dot(dz1, reduce_w.T, precision=lax.Precision.HIGHEST)
    return (gate, dpool)


def body(
    block_input,
    saved_maps,
    grad_p5,
    grad_p6,
    grad_p7,
    lateral,
    stacked,
    kernel,
    se_reduce,
    se_expand,
):
    rows_here = block_input.shape[1]
    cols = block_input.shape[2]
    cin = block_input.shape[3]
    wide = saved_maps.shape[-1]
    cells_here = rows_here * cols
    row_count = lax.axis_size("rows")
    cells = cells_here * row_count
    images = block_input.shape[0] * lax.axis_size("dp")
    flat = gather_streams(stacked[0].reshape(16, -1), GATHER_ROUNDS, [254])
    weight = flat.reshape(cin, wide)
    segment = lax.axis_index("segment")
    held = saved_maps[0, 0]
    image = block_input[0]
    taps = kernel.astype(jnp.float32)
    reduce_w = se_reduce.astype(jnp.float32)
    expand_w = se_expand.astype(jnp.float32)

    def rise_branch():
        return jax.nn.silu(held.astype(jnp.float32)).astype(jnp.bfloat16)

    def rise_still():
        return jnp.zeros((rows_here, cols, wide), jnp.bfloat16)

    expanded = lax.cond(segment == 1, rise_branch, rise_still)
    padded_e = margin(expanded)

    def pool_branch():
        dwo = depth_forward(padded_e, taps, rows_here, cols)
        act = jax.nn.silu(dwo)
        return (dwo, act, jnp.sum(act, axis=(0, 1)))

    def still_branch():
        return (
            jnp.zeros((rows_here, cols, wide), jnp.float32),
            jnp.zeros((rows_here, cols, wide), jnp.float32),
            jnp.zeros((wide,), jnp.float32),
        )

    dwo, act, pool_part = lax.cond(segment == 1, pool_branch, still_branch)

    def head_branch():
        inner = grad_p6[0].astype(jnp.float32) + up_two(grad_p7[0].astype(jnp.float32)) / 4.0
        g = (grad_p5[0].astype(jnp.float32) + up_two(inner) / 4.0).astype(jnp.bfloat16)
        grad_out = jnp.dot(
            g.reshape(cells_here, -1), lateral.T, preferred_element_type=jnp.float32
        ).astype(jnp.bfloat16)
        grad_proj = jnp.dot(grad_out, weight, preferred_element_type=jnp.float32).astype(
            jnp.bfloat16
        )
        term = jnp.dot(
            grad_out.T, held.reshape(cells_here, wide), preferred_element_type=jnp.float32
        )
        return (
            grad_out.reshape(rows_here, cols, cin),
            grad_proj.reshape(rows_here, cols, wide),
            term,
        )

    def head_still():
        return (
            jnp.zeros((rows_here, cols, cin), jnp.bfloat16),
            jnp.zeros((rows_here, cols, wide), jnp.bfloat16),
            jnp.zeros((cin, wide), jnp.float32),
        )

    grad_top, grad_proj, head_term = lax.cond(segment == 0, head_branch, head_still)
    shards = lax.axis_size("dp") * row_count
    chunk = cin * wide // shards

    def spread(term):
        flat_term = (term / images).reshape(shards, 8, -1)
        return scatter_streams(flat_term, SCATTER_ROUNDS, [512])

    def spread_still(term):
        return jnp.zeros((chunk,), jnp.float32)

    sent_top, sent_mid = passed_along((grad_top, grad_proj), "segment", 1)
    sent_top, sent_mid, head_term = lax.optimization_barrier((sent_top, sent_mid, head_term))
    head_share = lax.cond(segment == 0, spread, spread_still, head_term)
    head_share, sent_top, sent_mid, act = lax.optimization_barrier(
        (head_share, sent_top, sent_mid, act)
    )
    grad_part = jnp.sum(sent_mid.astype(jnp.float32) * act, axis=(0, 1))
    pool_total, grad_total = rows_sum((pool_part, grad_part))

    def gate_branch():
        gate, dpool = squeeze_gate(pool_total, grad_total, cells, reduce_w, expand_w)
        return ((sent_mid.astype(jnp.float32) * gate + dpool / cells) * silu_slope(dwo)).astype(
            jnp.bfloat16
        )

    def quiet_branch():
        return jnp.zeros((rows_here, cols, wide), jnp.bfloat16)

    grad_dw = lax.cond(segment == 1, gate_branch, quiet_branch)
    padded_grad = margin(grad_dw)

    def tail_branch():
        grad_e = depth_backward(padded_grad, taps, rows_here, cols)
        grad_pre = (
            (grad_e * silu_slope(held.astype(jnp.float32)))
            .astype(jnp.bfloat16)
            .reshape(cells_here, wide)
        )
        term = jnp.dot(
            image.reshape(cells_here, cin).T, grad_pre, preferred_element_type=jnp.float32
        )
        back = jnp.dot(grad_pre, weight.T, preferred_element_type=jnp.float32)
        grad_x = (sent_top.reshape(cells_here, cin).astype(jnp.float32) + back).astype(jnp.bfloat16)
        return (grad_x.reshape(rows_here, cols, cin), spread(term))

    def head_keep():
        return (grad_top, head_share)

    grad_here, share = lax.cond(segment == 1, tail_branch, head_keep)
    return (grad_here[None, None], share[None])


def solution(mesh):
    in_specs = (
        P("dp", "rows", None, None),
        P("segment", "dp", "rows", None, None),
        P("dp", "rows", None, None),
        P("dp", "rows", None, None),
        P("dp", "rows", None, None),
        P(),
        P("segment", ("dp", "rows")),
        P(),
        P(),
        P(),
    )
    out_specs = (P("segment", "dp", "rows", None, None), P("segment", ("dp", "rows")))
    return jax.shard_map(body, mesh=mesh, in_specs=in_specs, out_specs=out_specs, check_vma=False)
```

```python
import jax
import jax.numpy as jnp
from jax import lax
from jax.sharding import PartitionSpec as P


def extended_2(block, sides, width):
    for axis, dim in sides:
        count = lax.axis_size(axis)
        forward = [(i, i + 1) for i in range(count - 1)]
        backward = [(target, source) for source, target in forward]
        low = lax.ppermute(
            lax.slice_in_dim(block, block.shape[dim] - width, None, axis=dim), axis, forward
        )
        high = lax.ppermute(lax.slice_in_dim(block, 0, width, axis=dim), axis, backward)
        block = jnp.concatenate([low, block, high], axis=dim)
    return block


def passed_along(array, axis, by):
    length = lax.axis_size(axis)
    pairs = [(i, i + by) for i in range(length) if 0 <= i + by < length]
    return lax.ppermute(array, axis, pairs)


def flat_bits():
    rows_bits = lax.axis_size("rows").bit_length() - 1
    dp_bits = lax.axis_size("dp").bit_length() - 1
    return [("rows", k) for k in range(rows_bits)] + [("dp", k) for k in range(dp_bits)]


def swap_pairs(axis, j):
    return [(i, i ^ (1 << j)) for i in range(lax.axis_size(axis))]


def gather_chunks(piece, order):
    bits = flat_bits()
    buf = piece
    lead = []
    for axis, j in order:
        recv = lax.ppermute(buf, axis, swap_pairs(axis, j))
        high = (lax.axis_index(axis) >> j) & 1
        buf = jnp.stack([jnp.where(high == 0, buf, recv), jnp.where(high == 0, recv, buf)])
        lead.insert(0, bits.index((axis, j)))
    count = len(bits)
    perm = [lead.index(k) for k in reversed(range(count))] + [count, count + 1]
    return jnp.transpose(buf, perm).reshape((2**count,) + piece.shape)


def gather_streams(piece, orders, cuts):
    parts = jnp.split(piece, cuts, axis=-1)
    done = [gather_chunks(part, order) for part, order in zip(parts, orders)]
    return jnp.concatenate(done, axis=-1).reshape(-1)


def scatter_chunks(full, order):
    bits = flat_bits()
    count = len(bits)
    buf = full.reshape((2,) * count + full.shape[1:])
    live = list(reversed(range(count)))
    for axis, j in order:
        at = live.index(bits.index((axis, j)))
        high = (lax.axis_index(axis) >> j) & 1
        mine = lax.dynamic_index_in_dim(buf, high, at, keepdims=False)
        other = lax.dynamic_index_in_dim(buf, 1 - high, at, keepdims=False)
        buf = mine + lax.ppermute(other, axis, swap_pairs(axis, j))
        live.pop(at)
    return buf


def scatter_streams(full, orders, cuts):
    parts = jnp.split(full, cuts, axis=-1)
    done = [scatter_chunks(part, order) for part, order in zip(parts, orders)]
    return jnp.concatenate(done, axis=-1).reshape(-1)


def rows_sum(values):
    total = jnp.stack(values)
    for j in range(lax.axis_size("rows").bit_length() - 1):
        total = total + lax.ppermute(total, "rows", swap_pairs("rows", j))
    return tuple(total)


GATHER_ORDERS = (
    [("dp", 2), ("dp", 4), ("dp", 1), ("rows", 1), ("dp", 3), ("dp", 0), ("rows", 0)],
    [("dp", 4), ("rows", 1), ("dp", 2), ("dp", 1), ("rows", 0), ("dp", 3), ("dp", 0)],
)
SCATTER_ORDERS = tuple(order[::-1] for order in GATHER_ORDERS)


def up_two(v):
    return jnp.repeat(jnp.repeat(v, 2, axis=0), 2, axis=1)


def silu_slope(v):
    sig = jax.nn.sigmoid(v)
    return sig * (1.0 + v * (1.0 - sig))


def depth_forward(padded, taps, rows, cols):
    total = jnp.zeros((rows, cols, taps.shape[1]), jnp.float32)
    for p in range(5):
        for q in range(5):
            total = total + taps[5 * p + q] * padded[p : p + rows, q : q + cols].astype(jnp.float32)
    return total


def depth_backward(padded, taps, rows, cols):
    total = jnp.zeros((rows, cols, taps.shape[1]), jnp.float32)
    for p in range(5):
        for q in range(5):
            total = total + taps[5 * p + q] * padded[
                4 - p : 4 - p + rows, 4 - q : 4 - q + cols
            ].astype(jnp.float32)
    return total


def margin(values):
    extended = extended_2(values, (("rows", 0),), 2)
    return jnp.pad(extended, ((0, 0), (2, 2), (0, 0)))


def squeeze_gate(pool_total, grad_total, cells, reduce_w, expand_w):
    pooled = pool_total / cells
    z1 = jnp.dot(pooled, reduce_w, precision=lax.Precision.HIGHEST)
    z2 = jnp.dot(jax.nn.silu(z1), expand_w, precision=lax.Precision.HIGHEST)
    gate = jax.nn.sigmoid(z2)
    dz2 = grad_total * gate * (1.0 - gate)
    dz1 = jnp.dot(dz2, expand_w.T, precision=lax.Precision.HIGHEST) * silu_slope(z1)
    dpool = jnp.dot(dz1, reduce_w.T, precision=lax.Precision.HIGHEST)
    return (gate, dpool)


def body(
    block_input,
    saved_maps,
    grad_p5,
    grad_p6,
    grad_p7,
    lateral,
    stacked,
    kernel,
    se_reduce,
    se_expand,
):
    rows_here = block_input.shape[1]
    cols = block_input.shape[2]
    cin = block_input.shape[3]
    wide = saved_maps.shape[-1]
    cells_here = rows_here * cols
    row_count = lax.axis_size("rows")
    cells = cells_here * row_count
    images = block_input.shape[0] * lax.axis_size("dp")
    flat = gather_streams(stacked[0].reshape(16, -1), GATHER_ORDERS, [254])
    weight = flat.reshape(cin, wide)
    segment = lax.axis_index("segment")
    held = saved_maps[0, 0]
    image = block_input[0]
    taps = kernel.astype(jnp.float32)
    reduce_w = se_reduce.astype(jnp.float32)
    expand_w = se_expand.astype(jnp.float32)

    def rise_branch():
        return jax.nn.silu(held.astype(jnp.float32)).astype(jnp.bfloat16)

    def rise_still():
        return jnp.zeros((rows_here, cols, wide), jnp.bfloat16)

    expanded = lax.cond(segment == 1, rise_branch, rise_still)
    padded_e = margin(expanded)

    def pool_branch():
        dwo = depth_forward(padded_e, taps, rows_here, cols)
        act = jax.nn.silu(dwo)
        return (dwo, act, jnp.sum(act, axis=(0, 1)))

    def still_branch():
        return (
            jnp.zeros((rows_here, cols, wide), jnp.float32),
            jnp.zeros((rows_here, cols, wide), jnp.float32),
            jnp.zeros((wide,), jnp.float32),
        )

    dwo, act, pool_part = lax.cond(segment == 1, pool_branch, still_branch)

    def lead_branch():
        inner = grad_p6[0].astype(jnp.float32) + up_two(grad_p7[0].astype(jnp.float32)) / 4.0
        g = (grad_p5[0].astype(jnp.float32) + up_two(inner) / 4.0).astype(jnp.bfloat16)
        return jnp.dot(
            g.reshape(cells_here, -1), lateral.T, preferred_element_type=jnp.float32
        ).astype(jnp.bfloat16)

    def lead_still():
        return jnp.zeros((cells_here, cin), jnp.bfloat16)

    grad_out = lax.cond(segment == 0, lead_branch, lead_still)

    def head_branch():
        return jnp.dot(grad_out, weight, preferred_element_type=jnp.float32).astype(jnp.bfloat16)

    def head_still():
        return jnp.zeros((cells_here, wide), jnp.bfloat16)

    grad_proj = lax.cond(segment == 0, head_branch, head_still).reshape(rows_here, cols, wide)
    grad_top = grad_out.reshape(rows_here, cols, cin)
    shards = lax.axis_size("dp") * row_count
    chunk = cin * wide // shards

    def spread(term):
        flat_term = (term / images).reshape(shards, 8, -1)
        return scatter_streams(flat_term, SCATTER_ORDERS, [512])

    def spread_still(term):
        return jnp.zeros((chunk,), jnp.float32)

    sent_top, sent_mid = passed_along((grad_top, grad_proj), "segment", 1)
    sent_top, sent_mid, grad_out = lax.optimization_barrier((sent_top, sent_mid, grad_out))

    def term_branch():
        return jnp.dot(
            grad_out.T, held.reshape(cells_here, wide), preferred_element_type=jnp.float32
        )

    def term_still():
        return jnp.zeros((cin, wide), jnp.float32)

    head_term = lax.cond(segment == 0, term_branch, term_still)
    head_share = lax.cond(segment == 0, spread, spread_still, head_term)
    head_share, sent_top, sent_mid, act = lax.optimization_barrier(
        (head_share, sent_top, sent_mid, act)
    )
    grad_part = jnp.sum(sent_mid.astype(jnp.float32) * act, axis=(0, 1))
    pool_total, grad_total = rows_sum((pool_part, grad_part))

    def gate_branch():
        gate, dpool = squeeze_gate(pool_total, grad_total, cells, reduce_w, expand_w)
        return ((sent_mid.astype(jnp.float32) * gate + dpool / cells) * silu_slope(dwo)).astype(
            jnp.bfloat16
        )

    def quiet_branch():
        return jnp.zeros((rows_here, cols, wide), jnp.bfloat16)

    grad_dw = lax.cond(segment == 1, gate_branch, quiet_branch)
    padded_grad = margin(grad_dw)

    def tail_branch():
        grad_e = depth_backward(padded_grad, taps, rows_here, cols)
        grad_pre = (
            (grad_e * silu_slope(held.astype(jnp.float32)))
            .astype(jnp.bfloat16)
            .reshape(cells_here, wide)
        )
        term = jnp.dot(
            image.reshape(cells_here, cin).T, grad_pre, preferred_element_type=jnp.float32
        )
        back = jnp.dot(grad_pre, weight.T, preferred_element_type=jnp.float32)
        grad_x = (sent_top.reshape(cells_here, cin).astype(jnp.float32) + back).astype(jnp.bfloat16)
        return (grad_x.reshape(rows_here, cols, cin), spread(term))

    def head_keep():
        return (grad_top, head_share)

    grad_here, share = lax.cond(segment == 1, tail_branch, head_keep)
    return (grad_here[None, None], share[None])


def solution(mesh):
    in_specs = (
        P("dp", "rows", None, None),
        P("segment", "dp", "rows", None, None),
        P("dp", "rows", None, None),
        P("dp", "rows", None, None),
        P("dp", "rows", None, None),
        P(),
        P("segment", ("dp", "rows")),
        P(),
        P(),
        P(),
    )
    out_specs = (P("segment", "dp", "rows", None, None), P("segment", ("dp", "rows")))
    return jax.shard_map(body, mesh=mesh, in_specs=in_specs, out_specs=out_specs, check_vma=False)
```

```python
import jax
import jax.numpy as jnp
from jax import lax
from jax.sharding import PartitionSpec as P


def extended_2(block, sides, width):
    for axis, dim in sides:
        count = lax.axis_size(axis)
        forward = [(i, i + 1) for i in range(count - 1)]
        backward = [(target, source) for source, target in forward]
        low = lax.ppermute(
            lax.slice_in_dim(block, block.shape[dim] - width, None, axis=dim), axis, forward
        )
        high = lax.ppermute(lax.slice_in_dim(block, 0, width, axis=dim), axis, backward)
        block = jnp.concatenate([low, block, high], axis=dim)
    return block


def passed_along(array, axis, by):
    length = lax.axis_size(axis)
    pairs = [(i, i + by) for i in range(length) if 0 <= i + by < length]
    return lax.ppermute(array, axis, pairs)


def flat_bits():
    rows_bits = lax.axis_size("rows").bit_length() - 1
    dp_bits = lax.axis_size("dp").bit_length() - 1
    return [("rows", k) for k in range(rows_bits)] + [("dp", k) for k in range(dp_bits)]


def swap_pairs(axis, j):
    return [(i, i ^ (1 << j)) for i in range(lax.axis_size(axis))]


def gather_steps(buf, lead, order):
    bits = flat_bits()
    for axis, j in order:
        recv = lax.ppermute(buf, axis, swap_pairs(axis, j))
        high = (lax.axis_index(axis) >> j) & 1
        buf = jnp.stack([jnp.where(high == 0, buf, recv), jnp.where(high == 0, recv, buf)])
        lead = [bits.index((axis, j))] + lead
    return buf, lead


def gather_natural(buf, lead):
    count = len(lead)
    perm = [lead.index(k) for k in reversed(range(count))]
    perm += list(range(count, buf.ndim))
    return jnp.transpose(buf, perm).reshape((2**count,) + buf.shape[count:])


def gather_all(piece, common, orders, cuts):
    buf, lead = gather_steps(piece, [], common)
    parts = jnp.split(buf, cuts, axis=-1)
    done = [gather_natural(*gather_steps(part, lead, order)) for part, order in zip(parts, orders)]
    return jnp.concatenate(done, axis=-1).reshape(-1)


def scatter_steps(buf, live, order):
    bits = flat_bits()
    live = list(live)
    for axis, j in order:
        at = live.index(bits.index((axis, j)))
        high = (lax.axis_index(axis) >> j) & 1
        mine = lax.dynamic_index_in_dim(buf, high, at, keepdims=False)
        other = lax.dynamic_index_in_dim(buf, 1 - high, at, keepdims=False)
        buf = mine + lax.ppermute(other, axis, swap_pairs(axis, j))
        live.pop(at)
    return buf, live


def scatter_all(full, orders, cuts, common):
    count = len(flat_bits())
    buf = full.reshape((2,) * count + full.shape[1:])
    live = list(reversed(range(count)))
    parts = jnp.split(buf, cuts, axis=-1)
    done = [scatter_steps(part, live, order) for part, order in zip(parts, orders)]
    buf = jnp.concatenate([part for part, _ in done], axis=-1)
    buf, _ = scatter_steps(buf, done[0][1], common)
    return buf.reshape(-1)


def rows_sum(values):
    total = jnp.stack(values)
    for j in range(lax.axis_size("rows").bit_length() - 1):
        total = total + lax.ppermute(total, "rows", swap_pairs("rows", j))
    return tuple(total)


GATHER_COMMON = [("dp", 2), ("dp", 4), ("dp", 1), ("rows", 1), ("dp", 3)]
GATHER_ORDERS = ([("dp", 0), ("rows", 0)], [("rows", 0), ("dp", 0)])
SCATTER_ORDERS = tuple(order[::-1] for order in GATHER_ORDERS)
SCATTER_COMMON = GATHER_COMMON[::-1]


def up_two(v):
    return jnp.repeat(jnp.repeat(v, 2, axis=0), 2, axis=1)


def silu_slope(v):
    sig = jax.nn.sigmoid(v)
    return sig * (1.0 + v * (1.0 - sig))


def depth_forward(padded, taps, rows, cols):
    total = jnp.zeros((rows, cols, taps.shape[1]), jnp.float32)
    for p in range(5):
        for q in range(5):
            total = total + taps[5 * p + q] * padded[p : p + rows, q : q + cols].astype(jnp.float32)
    return total


def depth_backward(padded, taps, rows, cols):
    total = jnp.zeros((rows, cols, taps.shape[1]), jnp.float32)
    for p in range(5):
        for q in range(5):
            total = total + taps[5 * p + q] * padded[
                4 - p : 4 - p + rows, 4 - q : 4 - q + cols
            ].astype(jnp.float32)
    return total


def margin(values):
    extended = extended_2(values, (("rows", 0),), 2)
    return jnp.pad(extended, ((0, 0), (2, 2), (0, 0)))


def squeeze_gate(pool_total, grad_total, cells, reduce_w, expand_w):
    pooled = pool_total / cells
    z1 = jnp.dot(pooled, reduce_w, precision=lax.Precision.HIGHEST)
    z2 = jnp.dot(jax.nn.silu(z1), expand_w, precision=lax.Precision.HIGHEST)
    gate = jax.nn.sigmoid(z2)
    dz2 = grad_total * gate * (1.0 - gate)
    dz1 = jnp.dot(dz2, expand_w.T, precision=lax.Precision.HIGHEST) * silu_slope(z1)
    dpool = jnp.dot(dz1, reduce_w.T, precision=lax.Precision.HIGHEST)
    return (gate, dpool)


def body(
    block_input,
    saved_maps,
    grad_p5,
    grad_p6,
    grad_p7,
    lateral,
    stacked,
    kernel,
    se_reduce,
    se_expand,
):
    rows_here = block_input.shape[1]
    cols = block_input.shape[2]
    cin = block_input.shape[3]
    wide = saved_maps.shape[-1]
    cells_here = rows_here * cols
    row_count = lax.axis_size("rows")
    cells = cells_here * row_count
    images = block_input.shape[0] * lax.axis_size("dp")
    flat = gather_all(stacked[0].reshape(16, -1), GATHER_COMMON, GATHER_ORDERS, [254])
    weight = flat.reshape(cin, wide)
    segment = lax.axis_index("segment")
    held = saved_maps[0, 0]
    image = block_input[0]
    taps = kernel.astype(jnp.float32)
    reduce_w = se_reduce.astype(jnp.float32)
    expand_w = se_expand.astype(jnp.float32)

    def rise_branch():
        return jax.nn.silu(held.astype(jnp.float32)).astype(jnp.bfloat16)

    def rise_still():
        return jnp.zeros((rows_here, cols, wide), jnp.bfloat16)

    expanded = lax.cond(segment == 1, rise_branch, rise_still)
    padded_e = margin(expanded)

    def pool_branch():
        dwo = depth_forward(padded_e, taps, rows_here, cols)
        act = jax.nn.silu(dwo)
        return (dwo, act, jnp.sum(act, axis=(0, 1)))

    def still_branch():
        return (
            jnp.zeros((rows_here, cols, wide), jnp.float32),
            jnp.zeros((rows_here, cols, wide), jnp.float32),
            jnp.zeros((wide,), jnp.float32),
        )

    dwo, act, pool_part = lax.cond(segment == 1, pool_branch, still_branch)

    def lead_branch():
        inner = grad_p6[0].astype(jnp.float32) + up_two(grad_p7[0].astype(jnp.float32)) / 4.0
        g = (grad_p5[0].astype(jnp.float32) + up_two(inner) / 4.0).astype(jnp.bfloat16)
        return jnp.dot(
            g.reshape(cells_here, -1), lateral.T, preferred_element_type=jnp.float32
        ).astype(jnp.bfloat16)

    def lead_still():
        return jnp.zeros((cells_here, cin), jnp.bfloat16)

    grad_out = lax.cond(segment == 0, lead_branch, lead_still)

    def head_branch():
        return jnp.dot(grad_out, weight, preferred_element_type=jnp.float32).astype(jnp.bfloat16)

    def head_still():
        return jnp.zeros((cells_here, wide), jnp.bfloat16)

    grad_proj = lax.cond(segment == 0, head_branch, head_still).reshape(rows_here, cols, wide)
    grad_top = grad_out.reshape(rows_here, cols, cin)
    shards = lax.axis_size("dp") * row_count
    chunk = cin * wide // shards

    def spread(term):
        flat_term = (term / images).reshape(shards, 8, -1)
        return scatter_all(flat_term, SCATTER_ORDERS, [512], SCATTER_COMMON)

    def spread_still(term):
        return jnp.zeros((chunk,), jnp.float32)

    sent_top, sent_mid = passed_along((grad_top, grad_proj), "segment", 1)
    sent_top, sent_mid, grad_out = lax.optimization_barrier((sent_top, sent_mid, grad_out))

    def term_branch():
        return jnp.dot(
            grad_out.T, held.reshape(cells_here, wide), preferred_element_type=jnp.float32
        )

    def term_still():
        return jnp.zeros((cin, wide), jnp.float32)

    head_term = lax.cond(segment == 0, term_branch, term_still)
    head_share = lax.cond(segment == 0, spread, spread_still, head_term)
    head_share, sent_top, sent_mid, act = lax.optimization_barrier(
        (head_share, sent_top, sent_mid, act)
    )
    grad_part = jnp.sum(sent_mid.astype(jnp.float32) * act, axis=(0, 1))
    pool_total, grad_total = rows_sum((pool_part, grad_part))

    def gate_branch():
        gate, dpool = squeeze_gate(pool_total, grad_total, cells, reduce_w, expand_w)
        return ((sent_mid.astype(jnp.float32) * gate + dpool / cells) * silu_slope(dwo)).astype(
            jnp.bfloat16
        )

    def quiet_branch():
        return jnp.zeros((rows_here, cols, wide), jnp.bfloat16)

    grad_dw = lax.cond(segment == 1, gate_branch, quiet_branch)
    padded_grad = margin(grad_dw)

    def tail_branch():
        grad_e = depth_backward(padded_grad, taps, rows_here, cols)
        grad_pre = (
            (grad_e * silu_slope(held.astype(jnp.float32)))
            .astype(jnp.bfloat16)
            .reshape(cells_here, wide)
        )
        term = jnp.dot(
            image.reshape(cells_here, cin).T, grad_pre, preferred_element_type=jnp.float32
        )
        back = jnp.dot(grad_pre, weight.T, preferred_element_type=jnp.float32)
        grad_x = (sent_top.reshape(cells_here, cin).astype(jnp.float32) + back).astype(jnp.bfloat16)
        return (grad_x.reshape(rows_here, cols, cin), spread(term))

    def head_keep():
        return (grad_top, head_share)

    grad_here, share = lax.cond(segment == 1, tail_branch, head_keep)
    return (grad_here[None, None], share[None])


def solution(mesh):
    in_specs = (
        P("dp", "rows", None, None),
        P("segment", "dp", "rows", None, None),
        P("dp", "rows", None, None),
        P("dp", "rows", None, None),
        P("dp", "rows", None, None),
        P(),
        P("segment", ("dp", "rows")),
        P(),
        P(),
        P(),
    )
    out_specs = (P("segment", "dp", "rows", None, None), P("segment", ("dp", "rows")))
    return jax.shard_map(body, mesh=mesh, in_specs=in_specs, out_specs=out_specs, check_vma=False)
```

```python
import jax
import jax.numpy as jnp
from jax import lax
from jax.sharding import PartitionSpec as P


def extended_2(block, sides, width):
    for axis, dim in sides:
        count = lax.axis_size(axis)
        forward = [(i, i + 1) for i in range(count - 1)]
        backward = [(target, source) for source, target in forward]
        low = lax.ppermute(
            lax.slice_in_dim(block, block.shape[dim] - width, None, axis=dim), axis, forward
        )
        high = lax.ppermute(lax.slice_in_dim(block, 0, width, axis=dim), axis, backward)
        block = jnp.concatenate([low, block, high], axis=dim)
    return block


def passed_along(array, axis, by):
    length = lax.axis_size(axis)
    pairs = [(i, i + by) for i in range(length) if 0 <= i + by < length]
    return lax.ppermute(array, axis, pairs)


def flat_bits():
    rows_bits = lax.axis_size("rows").bit_length() - 1
    dp_bits = lax.axis_size("dp").bit_length() - 1
    return [("rows", k) for k in range(rows_bits)] + [("dp", k) for k in range(dp_bits)]


def swap_pairs(axis, j):
    return [(i, i ^ (1 << j)) for i in range(lax.axis_size(axis))]


def gather_chunks(piece, order):
    bits = flat_bits()
    buf = piece
    lead = []
    for axis, j in order:
        recv = lax.ppermute(buf, axis, swap_pairs(axis, j))
        high = (lax.axis_index(axis) >> j) & 1
        buf = jnp.stack([jnp.where(high == 0, buf, recv), jnp.where(high == 0, recv, buf)])
        lead.insert(0, bits.index((axis, j)))
    count = len(bits)
    perm = [lead.index(k) for k in reversed(range(count))] + [count, count + 1]
    return jnp.transpose(buf, perm).reshape((2**count,) + piece.shape)


def gather_streams(piece, orders, cuts):
    parts = jnp.split(piece, cuts, axis=-1)
    done = [gather_chunks(part, order) for part, order in zip(parts, orders)]
    return jnp.concatenate(done, axis=-1).reshape(-1)


def scatter_chunks(full, order, narrow=2):
    bits = flat_bits()
    count = len(bits)
    buf = full.reshape((2,) * count + full.shape[1:])
    live = list(reversed(range(count)))
    for step, (axis, j) in enumerate(order):
        at = live.index(bits.index((axis, j)))
        high = (lax.axis_index(axis) >> j) & 1
        mine = lax.dynamic_index_in_dim(buf, high, at, keepdims=False)
        other = lax.dynamic_index_in_dim(buf, 1 - high, at, keepdims=False)
        shape = other.shape
        if step < narrow:
            other = other.reshape(shape[:-3] + (-1, shape[-1])).astype(jnp.bfloat16)
        moved = lax.ppermute(other, axis, swap_pairs(axis, j))
        buf = mine + moved.astype(jnp.float32).reshape(shape)
        live.pop(at)
    return buf


def scatter_streams(full, orders, cuts):
    parts = jnp.split(full, cuts, axis=-1)
    done = [scatter_chunks(part, order) for part, order in zip(parts, orders)]
    return jnp.concatenate(done, axis=-1).reshape(-1)


def rows_sum(values):
    total = jnp.stack(values)
    for j in range(lax.axis_size("rows").bit_length() - 1):
        total = total + lax.ppermute(total, "rows", swap_pairs("rows", j))
    return tuple(total)


GATHER_ORDERS = (
    [("dp", 2), ("dp", 4), ("dp", 1), ("rows", 1), ("dp", 3), ("dp", 0), ("rows", 0)],
    [("dp", 4), ("rows", 1), ("dp", 2), ("dp", 1), ("rows", 0), ("dp", 3), ("dp", 0)],
)
SCATTER_ORDERS = tuple(order[::-1] for order in GATHER_ORDERS)


def up_two(v):
    return jnp.repeat(jnp.repeat(v, 2, axis=0), 2, axis=1)


def silu_slope(v):
    sig = jax.nn.sigmoid(v)
    return sig * (1.0 + v * (1.0 - sig))


def depth_forward(padded, taps, rows, cols):
    total = jnp.zeros((rows, cols, taps.shape[1]), jnp.float32)
    for p in range(5):
        for q in range(5):
            total = total + taps[5 * p + q] * padded[p : p + rows, q : q + cols].astype(jnp.float32)
    return total


def depth_backward(padded, taps, rows, cols):
    total = jnp.zeros((rows, cols, taps.shape[1]), jnp.float32)
    for p in range(5):
        for q in range(5):
            total = total + taps[5 * p + q] * padded[
                4 - p : 4 - p + rows, 4 - q : 4 - q + cols
            ].astype(jnp.float32)
    return total


def margin(values):
    extended = extended_2(values, (("rows", 0),), 2)
    return jnp.pad(extended, ((0, 0), (2, 2), (0, 0)))


def squeeze_gate(pool_total, grad_total, cells, reduce_w, expand_w):
    pooled = pool_total / cells
    z1 = jnp.dot(pooled, reduce_w, precision=lax.Precision.HIGHEST)
    z2 = jnp.dot(jax.nn.silu(z1), expand_w, precision=lax.Precision.HIGHEST)
    gate = jax.nn.sigmoid(z2)
    dz2 = grad_total * gate * (1.0 - gate)
    dz1 = jnp.dot(dz2, expand_w.T, precision=lax.Precision.HIGHEST) * silu_slope(z1)
    dpool = jnp.dot(dz1, reduce_w.T, precision=lax.Precision.HIGHEST)
    return (gate, dpool)


def body(
    block_input,
    saved_maps,
    grad_p5,
    grad_p6,
    grad_p7,
    lateral,
    stacked,
    kernel,
    se_reduce,
    se_expand,
):
    rows_here = block_input.shape[1]
    cols = block_input.shape[2]
    cin = block_input.shape[3]
    wide = saved_maps.shape[-1]
    cells_here = rows_here * cols
    row_count = lax.axis_size("rows")
    cells = cells_here * row_count
    images = block_input.shape[0] * lax.axis_size("dp")
    flat = gather_streams(stacked[0].reshape(16, -1), GATHER_ORDERS, [254])
    weight = flat.reshape(cin, wide)
    segment = lax.axis_index("segment")
    held = saved_maps[0, 0]
    image = block_input[0]
    taps = kernel.astype(jnp.float32)
    reduce_w = se_reduce.astype(jnp.float32)
    expand_w = se_expand.astype(jnp.float32)

    def rise_branch():
        return jax.nn.silu(held.astype(jnp.float32)).astype(jnp.bfloat16)

    def rise_still():
        return jnp.zeros((rows_here, cols, wide), jnp.bfloat16)

    expanded = lax.cond(segment == 1, rise_branch, rise_still)
    padded_e = margin(expanded)

    def pool_branch():
        dwo = depth_forward(padded_e, taps, rows_here, cols)
        act = jax.nn.silu(dwo)
        return (dwo, act, jnp.sum(act, axis=(0, 1)))

    def still_branch():
        return (
            jnp.zeros((rows_here, cols, wide), jnp.float32),
            jnp.zeros((rows_here, cols, wide), jnp.float32),
            jnp.zeros((wide,), jnp.float32),
        )

    dwo, act, pool_part = lax.cond(segment == 1, pool_branch, still_branch)

    def lead_branch():
        inner = grad_p6[0].astype(jnp.float32) + up_two(grad_p7[0].astype(jnp.float32)) / 4.0
        g = (grad_p5[0].astype(jnp.float32) + up_two(inner) / 4.0).astype(jnp.bfloat16)
        return jnp.dot(
            g.reshape(cells_here, -1), lateral.T, preferred_element_type=jnp.float32
        ).astype(jnp.bfloat16)

    def lead_still():
        return jnp.zeros((cells_here, cin), jnp.bfloat16)

    grad_out = lax.cond(segment == 0, lead_branch, lead_still)

    def head_branch():
        return jnp.dot(grad_out, weight, preferred_element_type=jnp.float32).astype(jnp.bfloat16)

    def head_still():
        return jnp.zeros((cells_here, wide), jnp.bfloat16)

    grad_proj = lax.cond(segment == 0, head_branch, head_still).reshape(rows_here, cols, wide)
    grad_top = grad_out.reshape(rows_here, cols, cin)
    shards = lax.axis_size("dp") * row_count
    chunk = cin * wide // shards

    def spread(term):
        flat_term = (term / images).reshape(shards, 8, -1)
        return scatter_streams(flat_term, SCATTER_ORDERS, [512])

    def spread_still(term):
        return jnp.zeros((chunk,), jnp.float32)

    sent_top, sent_mid = passed_along((grad_top, grad_proj), "segment", 1)
    sent_top, sent_mid, grad_out = lax.optimization_barrier((sent_top, sent_mid, grad_out))

    def term_branch():
        return jnp.dot(
            grad_out.T, held.reshape(cells_here, wide), preferred_element_type=jnp.float32
        )

    def term_still():
        return jnp.zeros((cin, wide), jnp.float32)

    head_term = lax.cond(segment == 0, term_branch, term_still)
    head_share = lax.cond(segment == 0, spread, spread_still, head_term)
    head_share, sent_top, sent_mid, act = lax.optimization_barrier(
        (head_share, sent_top, sent_mid, act)
    )
    grad_part = jnp.sum(sent_mid.astype(jnp.float32) * act, axis=(0, 1))
    pool_total, grad_total = rows_sum((pool_part, grad_part))

    def gate_branch():
        gate, dpool = squeeze_gate(pool_total, grad_total, cells, reduce_w, expand_w)
        return ((sent_mid.astype(jnp.float32) * gate + dpool / cells) * silu_slope(dwo)).astype(
            jnp.bfloat16
        )

    def quiet_branch():
        return jnp.zeros((rows_here, cols, wide), jnp.bfloat16)

    grad_dw = lax.cond(segment == 1, gate_branch, quiet_branch)
    padded_grad = margin(grad_dw)

    def tail_branch():
        grad_e = depth_backward(padded_grad, taps, rows_here, cols)
        grad_pre = (
            (grad_e * silu_slope(held.astype(jnp.float32)))
            .astype(jnp.bfloat16)
            .reshape(cells_here, wide)
        )
        term = jnp.dot(
            image.reshape(cells_here, cin).T, grad_pre, preferred_element_type=jnp.float32
        )
        back = jnp.dot(grad_pre, weight.T, preferred_element_type=jnp.float32)
        grad_x = (sent_top.reshape(cells_here, cin).astype(jnp.float32) + back).astype(jnp.bfloat16)
        return (grad_x.reshape(rows_here, cols, cin), spread(term))

    def head_keep():
        return (grad_top, head_share)

    grad_here, share = lax.cond(segment == 1, tail_branch, head_keep)
    return (grad_here[None, None], share[None])


def solution(mesh):
    in_specs = (
        P("dp", "rows", None, None),
        P("segment", "dp", "rows", None, None),
        P("dp", "rows", None, None),
        P("dp", "rows", None, None),
        P("dp", "rows", None, None),
        P(),
        P("segment", ("dp", "rows")),
        P(),
        P(),
        P(),
    )
    out_specs = (P("segment", "dp", "rows", None, None), P("segment", ("dp", "rows")))
    return jax.shard_map(body, mesh=mesh, in_specs=in_specs, out_specs=out_specs, check_vma=False)
```

```python
import jax
import jax.numpy as jnp
from jax import lax
from jax.sharding import PartitionSpec as P


def extended_2(block, sides, width):
    for axis, dim in sides:
        count = lax.axis_size(axis)
        forward = [(i, i + 1) for i in range(count - 1)]
        backward = [(target, source) for source, target in forward]
        low = lax.ppermute(
            lax.slice_in_dim(block, block.shape[dim] - width, None, axis=dim), axis, forward
        )
        high = lax.ppermute(lax.slice_in_dim(block, 0, width, axis=dim), axis, backward)
        block = jnp.concatenate([low, block, high], axis=dim)
    return block


def passed_along(array, axis, by):
    length = lax.axis_size(axis)
    pairs = [(i, i + by) for i in range(length) if 0 <= i + by < length]
    return lax.ppermute(array, axis, pairs)


def flat_bits():
    rows_bits = lax.axis_size("rows").bit_length() - 1
    dp_bits = lax.axis_size("dp").bit_length() - 1
    return [("rows", k) for k in range(rows_bits)] + [("dp", k) for k in range(dp_bits)]


def swap_pairs(axis, j):
    return [(i, i ^ (1 << j)) for i in range(lax.axis_size(axis))]


def gather_chunks(piece, order):
    bits = flat_bits()
    buf = piece
    lead = []
    for axis, j in order:
        recv = lax.ppermute(buf, axis, swap_pairs(axis, j))
        high = (lax.axis_index(axis) >> j) & 1
        buf = jnp.stack([jnp.where(high == 0, buf, recv), jnp.where(high == 0, recv, buf)])
        lead.insert(0, bits.index((axis, j)))
    count = len(bits)
    perm = [lead.index(k) for k in reversed(range(count))] + [count, count + 1]
    return jnp.transpose(buf, perm).reshape((2**count,) + piece.shape)


def gather_streams(piece, orders, cuts):
    parts = jnp.split(piece, cuts, axis=-1)
    done = [gather_chunks(part, order) for part, order in zip(parts, orders)]
    return jnp.concatenate(done, axis=-1).reshape(-1)


def scatter_chunks(full, order, narrow=2):
    bits = flat_bits()
    count = len(bits)
    buf = full.reshape((2,) * count + full.shape[1:])
    live = list(reversed(range(count)))
    for step, (axis, j) in enumerate(order):
        at = live.index(bits.index((axis, j)))
        high = (lax.axis_index(axis) >> j) & 1
        mine = lax.dynamic_index_in_dim(buf, high, at, keepdims=False)
        other = lax.dynamic_index_in_dim(buf, 1 - high, at, keepdims=False)
        shape = other.shape
        if step < narrow:
            other = other.reshape(shape[:-3] + (-1, shape[-1])).astype(jnp.bfloat16)
        moved = lax.ppermute(other, axis, swap_pairs(axis, j))
        buf = mine + moved.astype(jnp.float32).reshape(shape)
        live.pop(at)
    return buf


def scatter_streams(full, orders):
    done = [scatter_chunks(full[:, k], order) for k, order in enumerate(orders)]
    return jnp.stack(done).reshape(-1)


def rows_sum(values):
    total = jnp.stack(values)
    for j in range(lax.axis_size("rows").bit_length() - 1):
        total = total + lax.ppermute(total, "rows", swap_pairs("rows", j))
    return tuple(total)


GATHER_ORDERS = (
    [("dp", 2), ("dp", 4), ("dp", 1), ("rows", 1), ("dp", 3), ("dp", 0), ("rows", 0)],
    [("dp", 4), ("rows", 1), ("dp", 2), ("dp", 1), ("rows", 0), ("dp", 3), ("dp", 0)],
)
SCATTER_ORDERS = tuple(order[::-1] for order in GATHER_ORDERS)


def up_two(v):
    return jnp.repeat(jnp.repeat(v, 2, axis=0), 2, axis=1)


def silu_slope(v):
    sig = jax.nn.sigmoid(v)
    return sig * (1.0 + v * (1.0 - sig))


def depth_forward(padded, taps, rows, cols):
    total = jnp.zeros((rows, cols, taps.shape[1]), jnp.float32)
    for p in range(5):
        for q in range(5):
            total = total + taps[5 * p + q] * padded[p : p + rows, q : q + cols].astype(jnp.float32)
    return total


def depth_backward(padded, taps, rows, cols):
    total = jnp.zeros((rows, cols, taps.shape[1]), jnp.float32)
    for p in range(5):
        for q in range(5):
            total = total + taps[5 * p + q] * padded[
                4 - p : 4 - p + rows, 4 - q : 4 - q + cols
            ].astype(jnp.float32)
    return total


def margin(values):
    extended = extended_2(values, (("rows", 0),), 2)
    return jnp.pad(extended, ((0, 0), (2, 2), (0, 0)))


def squeeze_gate(pool_total, grad_total, cells, reduce_w, expand_w):
    pooled = pool_total / cells
    z1 = jnp.dot(pooled, reduce_w, precision=lax.Precision.HIGHEST)
    z2 = jnp.dot(jax.nn.silu(z1), expand_w, precision=lax.Precision.HIGHEST)
    gate = jax.nn.sigmoid(z2)
    dz2 = grad_total * gate * (1.0 - gate)
    dz1 = jnp.dot(dz2, expand_w.T, precision=lax.Precision.HIGHEST) * silu_slope(z1)
    dpool = jnp.dot(dz1, reduce_w.T, precision=lax.Precision.HIGHEST)
    return (gate, dpool)


def body(
    block_input,
    saved_maps,
    grad_p5,
    grad_p6,
    grad_p7,
    lateral,
    stacked,
    kernel,
    se_reduce,
    se_expand,
):
    rows_here = block_input.shape[1]
    cols = block_input.shape[2]
    cin = block_input.shape[3]
    wide = saved_maps.shape[-1]
    cells_here = rows_here * cols
    row_count = lax.axis_size("rows")
    cells = cells_here * row_count
    images = block_input.shape[0] * lax.axis_size("dp")
    flat = gather_streams(stacked[0].reshape(16, -1), GATHER_ORDERS, [254])
    weight = flat.reshape(cin, wide)
    segment = lax.axis_index("segment")
    held = saved_maps[0, 0]
    image = block_input[0]
    taps = kernel.astype(jnp.float32)
    reduce_w = se_reduce.astype(jnp.float32)
    expand_w = se_expand.astype(jnp.float32)

    def rise_branch():
        return jax.nn.silu(held.astype(jnp.float32)).astype(jnp.bfloat16)

    def rise_still():
        return jnp.zeros((rows_here, cols, wide), jnp.bfloat16)

    expanded = lax.cond(segment == 1, rise_branch, rise_still)
    padded_e = margin(expanded)

    def pool_branch():
        dwo = depth_forward(padded_e, taps, rows_here, cols)
        act = jax.nn.silu(dwo)
        return (dwo, act, jnp.sum(act, axis=(0, 1)))

    def still_branch():
        return (
            jnp.zeros((rows_here, cols, wide), jnp.float32),
            jnp.zeros((rows_here, cols, wide), jnp.float32),
            jnp.zeros((wide,), jnp.float32),
        )

    dwo, act, pool_part = lax.cond(segment == 1, pool_branch, still_branch)

    def lead_branch():
        inner = grad_p6[0].astype(jnp.float32) + up_two(grad_p7[0].astype(jnp.float32)) / 4.0
        g = (grad_p5[0].astype(jnp.float32) + up_two(inner) / 4.0).astype(jnp.bfloat16)
        return jnp.dot(
            g.reshape(cells_here, -1), lateral.T, preferred_element_type=jnp.float32
        ).astype(jnp.bfloat16)

    def lead_still():
        return jnp.zeros((cells_here, cin), jnp.bfloat16)

    grad_out = lax.cond(segment == 0, lead_branch, lead_still)

    def head_branch():
        return jnp.dot(grad_out, weight, preferred_element_type=jnp.float32).astype(jnp.bfloat16)

    def head_still():
        return jnp.zeros((cells_here, wide), jnp.bfloat16)

    grad_proj = lax.cond(segment == 0, head_branch, head_still).reshape(rows_here, cols, wide)
    grad_top = grad_out.reshape(rows_here, cols, cin)
    shards = lax.axis_size("dp") * row_count
    chunk = cin * wide // shards

    def spread(term):
        flat_term = (term / images).reshape(shards, len(SCATTER_ORDERS), 8, -1)
        return scatter_streams(flat_term, SCATTER_ORDERS)

    def spread_still(term):
        return jnp.zeros((chunk,), jnp.float32)

    sent_top, sent_mid = passed_along((grad_top, grad_proj), "segment", 1)
    sent_top, sent_mid, grad_out = lax.optimization_barrier((sent_top, sent_mid, grad_out))

    def term_branch():
        return jnp.dot(
            grad_out.T, held.reshape(cells_here, wide), preferred_element_type=jnp.float32
        )

    def term_still():
        return jnp.zeros((cin, wide), jnp.float32)

    head_term = lax.cond(segment == 0, term_branch, term_still)
    head_share = lax.cond(segment == 0, spread, spread_still, head_term)
    head_share, sent_top, sent_mid, act = lax.optimization_barrier(
        (head_share, sent_top, sent_mid, act)
    )
    grad_part = jnp.sum(sent_mid.astype(jnp.float32) * act, axis=(0, 1))
    pool_total, grad_total = rows_sum((pool_part, grad_part))

    def gate_branch():
        gate, dpool = squeeze_gate(pool_total, grad_total, cells, reduce_w, expand_w)
        return ((sent_mid.astype(jnp.float32) * gate + dpool / cells) * silu_slope(dwo)).astype(
            jnp.bfloat16
        )

    def quiet_branch():
        return jnp.zeros((rows_here, cols, wide), jnp.bfloat16)

    grad_dw = lax.cond(segment == 1, gate_branch, quiet_branch)
    padded_grad = margin(grad_dw)

    def tail_branch():
        grad_e = depth_backward(padded_grad, taps, rows_here, cols)
        grad_pre = (
            (grad_e * silu_slope(held.astype(jnp.float32)))
            .astype(jnp.bfloat16)
            .reshape(cells_here, wide)
        )
        term = jnp.dot(
            image.reshape(cells_here, cin).T, grad_pre, preferred_element_type=jnp.float32
        )
        back = jnp.dot(grad_pre, weight.T, preferred_element_type=jnp.float32)
        grad_x = (sent_top.reshape(cells_here, cin).astype(jnp.float32) + back).astype(jnp.bfloat16)
        return (grad_x.reshape(rows_here, cols, cin), spread(term))

    def head_keep():
        return (grad_top, head_share)

    grad_here, share = lax.cond(segment == 1, tail_branch, head_keep)
    return (grad_here[None, None], share[None])


def solution(mesh):
    in_specs = (
        P("dp", "rows", None, None),
        P("segment", "dp", "rows", None, None),
        P("dp", "rows", None, None),
        P("dp", "rows", None, None),
        P("dp", "rows", None, None),
        P(),
        P("segment", ("dp", "rows")),
        P(),
        P(),
        P(),
    )
    out_specs = (P("segment", "dp", "rows", None, None), P("segment", ("dp", "rows")))
    return jax.shard_map(body, mesh=mesh, in_specs=in_specs, out_specs=out_specs, check_vma=False)
```

```python
import jax
import jax.numpy as jnp
from jax import lax
from jax.sharding import PartitionSpec as P


def extended_2(block, sides, width):
    for axis, dim in sides:
        count = lax.axis_size(axis)
        forward = [(i, i + 1) for i in range(count - 1)]
        backward = [(target, source) for source, target in forward]
        low = lax.ppermute(
            lax.slice_in_dim(block, block.shape[dim] - width, None, axis=dim), axis, forward
        )
        high = lax.ppermute(lax.slice_in_dim(block, 0, width, axis=dim), axis, backward)
        block = jnp.concatenate([low, block, high], axis=dim)
    return block


def passed_along(array, axis, by):
    length = lax.axis_size(axis)
    pairs = [(i, i + by) for i in range(length) if 0 <= i + by < length]
    return lax.ppermute(array, axis, pairs)


def flat_bits():
    rows_bits = lax.axis_size("rows").bit_length() - 1
    dp_bits = lax.axis_size("dp").bit_length() - 1
    return [("rows", k) for k in range(rows_bits)] + [("dp", k) for k in range(dp_bits)]


def swap_pairs(axis, j):
    return [(i, i ^ (1 << j)) for i in range(lax.axis_size(axis))]


def gather_chunks(piece, order):
    bits = flat_bits()
    buf = piece
    lead = []
    for axis, j in order:
        recv = lax.ppermute(buf, axis, swap_pairs(axis, j))
        high = (lax.axis_index(axis) >> j) & 1
        buf = jnp.stack([jnp.where(high == 0, buf, recv), jnp.where(high == 0, recv, buf)])
        lead.insert(0, bits.index((axis, j)))
    count = len(bits)
    perm = [lead.index(k) for k in reversed(range(count))] + [count, count + 1]
    return jnp.transpose(buf, perm).reshape((2**count,) + piece.shape)


def gather_streams(piece, orders, cuts):
    parts = jnp.split(piece, cuts, axis=-1)
    done = [gather_chunks(part, order) for part, order in zip(parts, orders)]
    return jnp.concatenate(done, axis=-1).reshape(-1)


def scatter_chunks(full, order, narrow=2):
    bits = flat_bits()
    count = len(bits)
    buf = full.reshape((2,) * count + full.shape[1:])
    live = list(reversed(range(count)))
    for step, (axis, j) in enumerate(order):
        at = live.index(bits.index((axis, j)))
        high = (lax.axis_index(axis) >> j) & 1
        mine = lax.dynamic_index_in_dim(buf, high, at, keepdims=False)
        other = lax.dynamic_index_in_dim(buf, 1 - high, at, keepdims=False)
        shape = other.shape
        if step < narrow:
            other = other.reshape(shape[:-3] + (-1, shape[-1])).astype(jnp.bfloat16)
        moved = lax.ppermute(other, axis, swap_pairs(axis, j))
        buf = mine + moved.astype(jnp.float32).reshape(shape)
        live.pop(at)
    return buf


def scatter_streams(full, orders):
    done = [scatter_chunks(full[:, k], order) for k, order in enumerate(orders)]
    return jnp.stack(done).reshape(-1)


def rows_sum(values):
    total = jnp.stack(values)
    for j in range(lax.axis_size("rows").bit_length() - 1):
        total = total + lax.ppermute(total, "rows", swap_pairs("rows", j))
    return tuple(total)


GATHER_ORDERS = (
    [("dp", 2), ("dp", 4), ("dp", 1), ("rows", 1), ("dp", 3), ("dp", 0), ("rows", 0)],
    [("dp", 4), ("rows", 1), ("dp", 2), ("dp", 1), ("rows", 0), ("dp", 3), ("dp", 0)],
)
SCATTER_ORDERS = tuple(order[::-1] for order in GATHER_ORDERS)


def up_two(v):
    return jnp.repeat(jnp.repeat(v, 2, axis=0), 2, axis=1)


def silu_slope(v):
    sig = jax.nn.sigmoid(v)
    return sig * (1.0 + v * (1.0 - sig))


def depth_forward(padded, taps, rows, cols):
    total = jnp.zeros((rows, cols, taps.shape[1]), jnp.float32)
    for p in range(5):
        for q in range(5):
            total = total + taps[5 * p + q] * padded[p : p + rows, q : q + cols].astype(jnp.float32)
    return total


def depth_backward(padded, taps, rows, cols):
    total = jnp.zeros((rows, cols, taps.shape[1]), jnp.float32)
    for p in range(5):
        for q in range(5):
            total = total + taps[5 * p + q] * padded[
                4 - p : 4 - p + rows, 4 - q : 4 - q + cols
            ].astype(jnp.float32)
    return total


def margin(values):
    extended = extended_2(values, (("rows", 0),), 2)
    return jnp.pad(extended, ((0, 0), (2, 2), (0, 0)))


def squeeze_gate(pool_total, grad_total, cells, reduce_w, expand_w):
    pooled = pool_total / cells
    z1 = jnp.dot(pooled, reduce_w, precision=lax.Precision.HIGHEST)
    z2 = jnp.dot(jax.nn.silu(z1), expand_w, precision=lax.Precision.HIGHEST)
    gate = jax.nn.sigmoid(z2)
    dz2 = grad_total * gate * (1.0 - gate)
    dz1 = jnp.dot(dz2, expand_w.T, precision=lax.Precision.HIGHEST) * silu_slope(z1)
    dpool = jnp.dot(dz1, reduce_w.T, precision=lax.Precision.HIGHEST)
    return (gate, dpool)


def body(
    block_input,
    saved_maps,
    grad_p5,
    grad_p6,
    grad_p7,
    lateral,
    stacked,
    kernel,
    se_reduce,
    se_expand,
):
    rows_here = block_input.shape[1]
    cols = block_input.shape[2]
    cin = block_input.shape[3]
    wide = saved_maps.shape[-1]
    cells_here = rows_here * cols
    row_count = lax.axis_size("rows")
    cells = cells_here * row_count
    images = block_input.shape[0] * lax.axis_size("dp")
    flat = gather_streams(stacked[0].reshape(16, -1), GATHER_ORDERS, [254])
    weight = flat.reshape(cin, wide)
    segment = lax.axis_index("segment")
    held = saved_maps[0, 0]
    image = block_input[0]
    taps = kernel.astype(jnp.float32)
    reduce_w = se_reduce.astype(jnp.float32)
    expand_w = se_expand.astype(jnp.float32)

    def rise_branch():
        return jax.nn.silu(held.astype(jnp.float32)).astype(jnp.bfloat16)

    def rise_still():
        return jnp.zeros((rows_here, cols, wide), jnp.bfloat16)

    expanded = lax.cond(segment == 1, rise_branch, rise_still)
    padded_e = margin(expanded)

    def pool_branch():
        dwo = depth_forward(padded_e, taps, rows_here, cols)
        act = jax.nn.silu(dwo)
        return (dwo, act, jnp.sum(act, axis=(0, 1)))

    def still_branch():
        return (
            jnp.zeros((rows_here, cols, wide), jnp.float32),
            jnp.zeros((rows_here, cols, wide), jnp.float32),
            jnp.zeros((wide,), jnp.float32),
        )

    dwo, act, pool_part = lax.cond(segment == 1, pool_branch, still_branch)

    def lead_branch():
        inner = grad_p6[0].astype(jnp.float32) + up_two(grad_p7[0].astype(jnp.float32)) / 4.0
        g = (grad_p5[0].astype(jnp.float32) + up_two(inner) / 4.0).astype(jnp.bfloat16)
        return jnp.dot(
            g.reshape(cells_here, -1), lateral.T, preferred_element_type=jnp.float32
        ).astype(jnp.bfloat16)

    def lead_still():
        return jnp.zeros((cells_here, cin), jnp.bfloat16)

    grad_out = lax.cond(segment == 0, lead_branch, lead_still)

    def head_branch():
        return jnp.dot(grad_out, weight, preferred_element_type=jnp.float32).astype(jnp.bfloat16)

    def head_still():
        return jnp.zeros((cells_here, wide), jnp.bfloat16)

    grad_proj = lax.cond(segment == 0, head_branch, head_still).reshape(rows_here, cols, wide)
    grad_top = grad_out.reshape(rows_here, cols, cin)
    shards = lax.axis_size("dp") * row_count
    chunk = cin * wide // shards

    def spread(term):
        flat_term = (term / images).reshape(shards, len(SCATTER_ORDERS), 8, -1)
        return scatter_streams(flat_term, SCATTER_ORDERS)

    def spread_still(term):
        return jnp.zeros((chunk,), jnp.float32)

    sent_top, sent_mid = passed_along((grad_top, grad_proj), "segment", 1)
    sent_top, sent_mid, grad_out = lax.optimization_barrier((sent_top, sent_mid, grad_out))

    def term_branch():
        return jnp.dot(
            grad_out.T, held.reshape(cells_here, wide), preferred_element_type=jnp.float32
        )

    def term_still():
        return jnp.zeros((cin, wide), jnp.float32)

    head_term = lax.cond(segment == 0, term_branch, term_still)
    head_share = lax.cond(segment == 0, spread, spread_still, head_term)
    head_share, sent_top, sent_mid, act = lax.optimization_barrier(
        (head_share, sent_top, sent_mid, act)
    )
    grad_part = jnp.sum(sent_mid.astype(jnp.float32) * act, axis=(0, 1))
    pool_total, grad_total = rows_sum((pool_part, grad_part))

    mid_rows = extended_2(sent_mid, (("rows", 0),), 2)
    dwo_rows = extended_2(dwo, (("rows", 0),), 2)
    row_at = lax.axis_index("rows") * rows_here - 2 + jnp.arange(rows_here + 4)
    inside = ((row_at >= 0) & (row_at < rows_here * row_count))[:, None, None]

    def gate_branch():
        gate, dpool = squeeze_gate(pool_total, grad_total, cells, reduce_w, expand_w)
        full = (mid_rows.astype(jnp.float32) * gate + dpool / cells) * silu_slope(dwo_rows)
        return jnp.where(inside, full, 0.0).astype(jnp.bfloat16)

    def quiet_branch():
        return jnp.zeros((rows_here + 4, cols, wide), jnp.bfloat16)

    grad_rows = lax.cond(segment == 1, gate_branch, quiet_branch)
    padded_grad = jnp.pad(grad_rows, ((0, 0), (2, 2), (0, 0)))

    def tail_branch():
        grad_e = depth_backward(padded_grad, taps, rows_here, cols)
        grad_pre = (
            (grad_e * silu_slope(held.astype(jnp.float32)))
            .astype(jnp.bfloat16)
            .reshape(cells_here, wide)
        )
        term = jnp.dot(
            image.reshape(cells_here, cin).T, grad_pre, preferred_element_type=jnp.float32
        )
        back = jnp.dot(grad_pre, weight.T, preferred_element_type=jnp.float32)
        grad_x = (sent_top.reshape(cells_here, cin).astype(jnp.float32) + back).astype(jnp.bfloat16)
        return (grad_x.reshape(rows_here, cols, cin), spread(term))

    def head_keep():
        return (grad_top, head_share)

    grad_here, share = lax.cond(segment == 1, tail_branch, head_keep)
    return (grad_here[None, None], share[None])


def solution(mesh):
    in_specs = (
        P("dp", "rows", None, None),
        P("segment", "dp", "rows", None, None),
        P("dp", "rows", None, None),
        P("dp", "rows", None, None),
        P("dp", "rows", None, None),
        P(),
        P("segment", ("dp", "rows")),
        P(),
        P(),
        P(),
    )
    out_specs = (P("segment", "dp", "rows", None, None), P("segment", ("dp", "rows")))
    return jax.shard_map(body, mesh=mesh, in_specs=in_specs, out_specs=out_specs, check_vma=False)
```

```python
import jax
import jax.numpy as jnp
from jax import lax
from jax.sharding import PartitionSpec as P


def extended_2(block, sides, width):
    for axis, dim in sides:
        count = lax.axis_size(axis)
        forward = [(i, i + 1) for i in range(count - 1)]
        backward = [(target, source) for source, target in forward]
        low = lax.ppermute(
            lax.slice_in_dim(block, block.shape[dim] - width, None, axis=dim), axis, forward
        )
        high = lax.ppermute(lax.slice_in_dim(block, 0, width, axis=dim), axis, backward)
        block = jnp.concatenate([low, block, high], axis=dim)
    return block


def passed_along(array, axis, by):
    length = lax.axis_size(axis)
    pairs = [(i, i + by) for i in range(length) if 0 <= i + by < length]
    return lax.ppermute(array, axis, pairs)


def flat_bits():
    rows_bits = lax.axis_size("rows").bit_length() - 1
    dp_bits = lax.axis_size("dp").bit_length() - 1
    return [("rows", k) for k in range(rows_bits)] + [("dp", k) for k in range(dp_bits)]


def swap_pairs(axis, j):
    return [(i, i ^ (1 << j)) for i in range(lax.axis_size(axis))]


def gather_chunks(piece, order):
    bits = flat_bits()
    buf = piece
    lead = []
    for axis, j in order:
        recv = lax.ppermute(buf, axis, swap_pairs(axis, j))
        high = (lax.axis_index(axis) >> j) & 1
        buf = jnp.stack([jnp.where(high == 0, buf, recv), jnp.where(high == 0, recv, buf)])
        lead.insert(0, bits.index((axis, j)))
    count = len(bits)
    perm = [lead.index(k) for k in reversed(range(count))] + [count, count + 1]
    return jnp.transpose(buf, perm).reshape((2**count,) + piece.shape)


def gather_streams(piece, orders, cuts):
    parts = jnp.split(piece, cuts, axis=-1)
    done = [gather_chunks(part, order) for part, order in zip(parts, orders)]
    return jnp.concatenate(done, axis=-1).reshape(-1)


def scatter_chunks(full, order, narrow=2):
    bits = flat_bits()
    count = len(bits)
    buf = full.reshape((2,) * count + full.shape[1:])
    live = list(reversed(range(count)))
    for step, (axis, j) in enumerate(order):
        at = live.index(bits.index((axis, j)))
        high = (lax.axis_index(axis) >> j) & 1
        mine = lax.dynamic_index_in_dim(buf, high, at, keepdims=False)
        other = lax.dynamic_index_in_dim(buf, 1 - high, at, keepdims=False)
        shape = other.shape
        if step < narrow:
            other = other.reshape(shape[:-3] + (-1, shape[-1])).astype(jnp.bfloat16)
        moved = lax.ppermute(other, axis, swap_pairs(axis, j))
        buf = mine + moved.astype(jnp.float32).reshape(shape)
        live.pop(at)
    return buf


def scatter_streams(full, orders, cuts):
    parts = jnp.split(full, cuts, axis=-1)
    done = [scatter_chunks(part, order) for part, order in zip(parts, orders)]
    return jnp.concatenate(done, axis=-1).reshape(-1)


def rows_sum(values):
    total = jnp.stack(values)
    for j in range(lax.axis_size("rows").bit_length() - 1):
        total = total + lax.ppermute(total, "rows", swap_pairs("rows", j))
    return tuple(total)


GATHER_ORDERS = (
    [("dp", 2), ("dp", 4), ("dp", 1), ("rows", 1), ("dp", 3), ("dp", 0), ("rows", 0)],
    [("dp", 4), ("rows", 1), ("dp", 2), ("dp", 1), ("rows", 0), ("dp", 3), ("dp", 0)],
)
SCATTER_ORDERS = tuple(order[::-1] for order in GATHER_ORDERS)


def up_two(v):
    return jnp.repeat(jnp.repeat(v, 2, axis=0), 2, axis=1)


def silu_slope(v):
    sig = jax.nn.sigmoid(v)
    return sig * (1.0 + v * (1.0 - sig))


def depth_forward(padded, taps, rows, cols):
    total = jnp.zeros((rows, cols, taps.shape[1]), jnp.float32)
    for p in range(5):
        for q in range(5):
            total = total + taps[5 * p + q] * padded[p : p + rows, q : q + cols].astype(jnp.float32)
    return total


def depth_backward(padded, taps, rows, cols):
    total = jnp.zeros((rows, cols, taps.shape[1]), jnp.float32)
    for p in range(5):
        for q in range(5):
            total = total + taps[5 * p + q] * padded[
                4 - p : 4 - p + rows, 4 - q : 4 - q + cols
            ].astype(jnp.float32)
    return total


def margin(values):
    extended = extended_2(values, (("rows", 0),), 2)
    return jnp.pad(extended, ((0, 0), (2, 2), (0, 0)))


def squeeze_gate(pool_total, grad_total, cells, reduce_w, expand_w):
    pooled = pool_total / cells
    z1 = jnp.dot(pooled, reduce_w, precision=lax.Precision.HIGHEST)
    z2 = jnp.dot(jax.nn.silu(z1), expand_w, precision=lax.Precision.HIGHEST)
    gate = jax.nn.sigmoid(z2)
    dz2 = grad_total * gate * (1.0 - gate)
    dz1 = jnp.dot(dz2, expand_w.T, precision=lax.Precision.HIGHEST) * silu_slope(z1)
    dpool = jnp.dot(dz1, reduce_w.T, precision=lax.Precision.HIGHEST)
    return (gate, dpool)


def body(
    block_input,
    saved_maps,
    grad_p5,
    grad_p6,
    grad_p7,
    lateral,
    stacked,
    kernel,
    se_reduce,
    se_expand,
):
    rows_here = block_input.shape[1]
    cols = block_input.shape[2]
    cin = block_input.shape[3]
    wide = saved_maps.shape[-1]
    cells_here = rows_here * cols
    row_count = lax.axis_size("rows")
    cells = cells_here * row_count
    images = block_input.shape[0] * lax.axis_size("dp")
    flat = gather_streams(stacked[0].reshape(16, -1), GATHER_ORDERS, [254])
    weight = flat.reshape(cin, wide)
    segment = lax.axis_index("segment")
    held = saved_maps[0, 0]
    image = block_input[0]
    taps = kernel.astype(jnp.float32)
    reduce_w = se_reduce.astype(jnp.float32)
    expand_w = se_expand.astype(jnp.float32)

    def rise_branch():
        return jax.nn.silu(held.astype(jnp.float32)).astype(jnp.bfloat16)

    def rise_still():
        return jnp.zeros((rows_here, cols, wide), jnp.bfloat16)

    expanded = lax.cond(segment == 1, rise_branch, rise_still)
    padded_e = margin(expanded)

    def pool_branch():
        dwo = depth_forward(padded_e, taps, rows_here, cols)
        act = jax.nn.silu(dwo)
        return (dwo, act, jnp.sum(act, axis=(0, 1)))

    def still_branch():
        return (
            jnp.zeros((rows_here, cols, wide), jnp.float32),
            jnp.zeros((rows_here, cols, wide), jnp.float32),
            jnp.zeros((wide,), jnp.float32),
        )

    dwo, act, pool_part = lax.cond(segment == 1, pool_branch, still_branch)

    def lead_branch():
        inner = grad_p6[0].astype(jnp.float32) + up_two(grad_p7[0].astype(jnp.float32)) / 4.0
        g = (grad_p5[0].astype(jnp.float32) + up_two(inner) / 4.0).astype(jnp.bfloat16)
        return jnp.dot(
            g.reshape(cells_here, -1), lateral.T, preferred_element_type=jnp.float32
        ).astype(jnp.bfloat16)

    def lead_still():
        return jnp.zeros((cells_here, cin), jnp.bfloat16)

    grad_out = lax.cond(segment == 0, lead_branch, lead_still)

    def head_branch():
        return jnp.dot(grad_out, weight, preferred_element_type=jnp.float32).astype(jnp.bfloat16)

    def head_still():
        return jnp.zeros((cells_here, wide), jnp.bfloat16)

    grad_proj = lax.cond(segment == 0, head_branch, head_still).reshape(rows_here, cols, wide)
    grad_top = grad_out.reshape(rows_here, cols, cin)
    shards = lax.axis_size("dp") * row_count

    def spread(term):
        flat_term = (term / images).reshape(shards, 8, -1)
        return scatter_streams(flat_term, SCATTER_ORDERS, [512])

    sent_top, sent_mid = passed_along((grad_top, grad_proj), "segment", 1)
    sent_top, sent_mid, grad_out = lax.optimization_barrier((sent_top, sent_mid, grad_out))

    def term_branch():
        return jnp.dot(
            grad_out.T, held.reshape(cells_here, wide), preferred_element_type=jnp.float32
        )

    def term_still():
        return jnp.zeros((cin, wide), jnp.float32)

    head_term = lax.cond(segment == 0, term_branch, term_still)
    grad_part = jnp.sum(sent_mid.astype(jnp.float32) * act, axis=(0, 1))
    pool_total, grad_total = rows_sum((pool_part, grad_part))

    def gate_branch():
        gate, dpool = squeeze_gate(pool_total, grad_total, cells, reduce_w, expand_w)
        return ((sent_mid.astype(jnp.float32) * gate + dpool / cells) * silu_slope(dwo)).astype(
            jnp.bfloat16
        )

    def quiet_branch():
        return jnp.zeros((rows_here, cols, wide), jnp.bfloat16)

    grad_dw = lax.cond(segment == 1, gate_branch, quiet_branch)
    padded_grad = margin(grad_dw)

    def tail_branch():
        grad_e = depth_backward(padded_grad, taps, rows_here, cols)
        grad_pre = (
            (grad_e * silu_slope(held.astype(jnp.float32)))
            .astype(jnp.bfloat16)
            .reshape(cells_here, wide)
        )
        term = jnp.dot(
            image.reshape(cells_here, cin).T, grad_pre, preferred_element_type=jnp.float32
        )
        back = jnp.dot(grad_pre, weight.T, preferred_element_type=jnp.float32)
        grad_x = (sent_top.reshape(cells_here, cin).astype(jnp.float32) + back).astype(jnp.bfloat16)
        return (grad_x.reshape(rows_here, cols, cin), term)

    def head_keep():
        return (grad_top, head_term)

    grad_here, term = lax.cond(segment == 1, tail_branch, head_keep)
    share = spread(term)
    return (grad_here[None, None], share[None])


def solution(mesh):
    in_specs = (
        P("dp", "rows", None, None),
        P("segment", "dp", "rows", None, None),
        P("dp", "rows", None, None),
        P("dp", "rows", None, None),
        P("dp", "rows", None, None),
        P(),
        P("segment", ("dp", "rows")),
        P(),
        P(),
        P(),
    )
    out_specs = (P("segment", "dp", "rows", None, None), P("segment", ("dp", "rows")))
    return jax.shard_map(body, mesh=mesh, in_specs=in_specs, out_specs=out_specs, check_vma=False)
```

```python
import jax
import jax.numpy as jnp
from jax import lax
from jax.sharding import PartitionSpec as P


def extended_2(block, sides, width):
    for axis, dim in sides:
        count = lax.axis_size(axis)
        forward = [(i, i + 1) for i in range(count - 1)]
        backward = [(target, source) for source, target in forward]
        low = lax.ppermute(
            lax.slice_in_dim(block, block.shape[dim] - width, None, axis=dim), axis, forward
        )
        high = lax.ppermute(lax.slice_in_dim(block, 0, width, axis=dim), axis, backward)
        block = jnp.concatenate([low, block, high], axis=dim)
    return block


def passed_along(array, axis, by):
    length = lax.axis_size(axis)
    pairs = [(i, i + by) for i in range(length) if 0 <= i + by < length]
    return lax.ppermute(array, axis, pairs)


def flat_bits():
    rows_bits = lax.axis_size("rows").bit_length() - 1
    dp_bits = lax.axis_size("dp").bit_length() - 1
    return [("rows", k) for k in range(rows_bits)] + [("dp", k) for k in range(dp_bits)]


def swap_pairs(axis, j):
    return [(i, i ^ (1 << j)) for i in range(lax.axis_size(axis))]


def gather_chunks(piece, order):
    bits = flat_bits()
    buf = piece
    lead = []
    for axis, j in order:
        recv = lax.ppermute(buf, axis, swap_pairs(axis, j))
        high = (lax.axis_index(axis) >> j) & 1
        buf = jnp.stack([jnp.where(high == 0, buf, recv), jnp.where(high == 0, recv, buf)])
        lead.insert(0, bits.index((axis, j)))
    count = len(bits)
    perm = [lead.index(k) for k in reversed(range(count))] + [count, count + 1]
    return jnp.transpose(buf, perm).reshape((2**count,) + piece.shape)


def gather_streams(piece, orders, cuts):
    parts = jnp.split(piece, cuts, axis=-1)
    done = [gather_chunks(part, order) for part, order in zip(parts, orders)]
    return jnp.concatenate(done, axis=-1).reshape(-1)


def scatter_chunks(full, order, narrow=2):
    bits = flat_bits()
    count = len(bits)
    buf = full.reshape((2,) * count + full.shape[1:])
    live = list(reversed(range(count)))
    for step, (axis, j) in enumerate(order):
        at = live.index(bits.index((axis, j)))
        high = (lax.axis_index(axis) >> j) & 1
        mine = lax.dynamic_index_in_dim(buf, high, at, keepdims=False)
        other = lax.dynamic_index_in_dim(buf, 1 - high, at, keepdims=False)
        shape = other.shape
        if step < narrow:
            other = other.reshape(shape[:-3] + (-1, shape[-1])).astype(jnp.bfloat16)
        moved = lax.ppermute(other, axis, swap_pairs(axis, j))
        buf = mine + moved.astype(jnp.float32).reshape(shape)
        live.pop(at)
    return buf


def scatter_streams(full, orders, cuts):
    parts = jnp.split(full, cuts, axis=-1)
    done = [scatter_chunks(part, order) for part, order in zip(parts, orders)]
    return jnp.concatenate(done, axis=-1).reshape(-1)


def rows_sum(values):
    total = jnp.stack(values)
    for j in range(lax.axis_size("rows").bit_length() - 1):
        total = total + lax.ppermute(total, "rows", swap_pairs("rows", j))
    return tuple(total)


GATHER_ORDERS = (
    [("dp", 2), ("dp", 4), ("dp", 1), ("rows", 1), ("dp", 3), ("dp", 0), ("rows", 0)],
    [("dp", 4), ("rows", 1), ("dp", 2), ("dp", 1), ("rows", 0), ("dp", 3), ("dp", 0)],
)
SCATTER_ORDERS = tuple(order[::-1] for order in GATHER_ORDERS)


def up_two(v):
    return jnp.repeat(jnp.repeat(v, 2, axis=0), 2, axis=1)


def silu_slope(v):
    sig = jax.nn.sigmoid(v)
    return sig * (1.0 + v * (1.0 - sig))


def depth_forward(padded, taps, rows, cols):
    total = jnp.zeros((rows, cols, taps.shape[1]), jnp.float32)
    for p in range(5):
        for q in range(5):
            total = total + taps[5 * p + q] * padded[p : p + rows, q : q + cols].astype(jnp.float32)
    return total


def depth_backward(padded, taps, rows, cols):
    total = jnp.zeros((rows, cols, taps.shape[1]), jnp.float32)
    for p in range(5):
        for q in range(5):
            total = total + taps[5 * p + q] * padded[
                4 - p : 4 - p + rows, 4 - q : 4 - q + cols
            ].astype(jnp.float32)
    return total


def margin(values):
    extended = extended_2(values, (("rows", 0),), 2)
    return jnp.pad(extended, ((0, 0), (2, 2), (0, 0)))


def squeeze_gate(pool_total, grad_total, cells, reduce_w, expand_w):
    pooled = pool_total / cells
    z1 = jnp.dot(pooled, reduce_w, precision=lax.Precision.HIGHEST)
    z2 = jnp.dot(jax.nn.silu(z1), expand_w, precision=lax.Precision.HIGHEST)
    gate = jax.nn.sigmoid(z2)
    dz2 = grad_total * gate * (1.0 - gate)
    dz1 = jnp.dot(dz2, expand_w.T, precision=lax.Precision.HIGHEST) * silu_slope(z1)
    dpool = jnp.dot(dz1, reduce_w.T, precision=lax.Precision.HIGHEST)
    return (gate, dpool)


def body(
    block_input,
    saved_maps,
    grad_p5,
    grad_p6,
    grad_p7,
    lateral,
    stacked,
    kernel,
    se_reduce,
    se_expand,
):
    rows_here = block_input.shape[1]
    cols = block_input.shape[2]
    cin = block_input.shape[3]
    wide = saved_maps.shape[-1]
    cells_here = rows_here * cols
    row_count = lax.axis_size("rows")
    cells = cells_here * row_count
    images = block_input.shape[0] * lax.axis_size("dp")
    flat = gather_streams(stacked[0].reshape(16, -1), GATHER_ORDERS, [254])
    weight = flat.reshape(cin, wide)
    segment = lax.axis_index("segment")
    held = saved_maps[0, 0]
    image = block_input[0]
    taps = kernel.astype(jnp.float32)
    reduce_w = se_reduce.astype(jnp.float32)
    expand_w = se_expand.astype(jnp.float32)

    def rise_branch():
        return jax.nn.silu(held.astype(jnp.float32)).astype(jnp.bfloat16)

    def rise_still():
        return jnp.zeros((rows_here, cols, wide), jnp.bfloat16)

    expanded = lax.cond(segment == 1, rise_branch, rise_still)
    padded_e = margin(expanded)

    def pool_branch():
        dwo = depth_forward(padded_e, taps, rows_here, cols)
        act = jax.nn.silu(dwo)
        return (dwo, act, jnp.sum(act, axis=(0, 1)))

    def still_branch():
        return (
            jnp.zeros((rows_here, cols, wide), jnp.float32),
            jnp.zeros((rows_here, cols, wide), jnp.float32),
            jnp.zeros((wide,), jnp.float32),
        )

    dwo, act, pool_part = lax.cond(segment == 1, pool_branch, still_branch)

    def lead_branch():
        inner = grad_p6[0].astype(jnp.float32) + up_two(grad_p7[0].astype(jnp.float32)) / 4.0
        g = (grad_p5[0].astype(jnp.float32) + up_two(inner) / 4.0).astype(jnp.bfloat16)
        return jnp.dot(
            g.reshape(cells_here, -1), lateral.T, preferred_element_type=jnp.float32
        ).astype(jnp.bfloat16)

    def lead_still():
        return jnp.zeros((cells_here, cin), jnp.bfloat16)

    grad_out = lax.cond(segment == 0, lead_branch, lead_still)

    def head_branch():
        return jnp.dot(grad_out, weight, preferred_element_type=jnp.float32).astype(jnp.bfloat16)

    def head_still():
        return jnp.zeros((cells_here, wide), jnp.bfloat16)

    grad_proj = lax.cond(segment == 0, head_branch, head_still).reshape(rows_here, cols, wide)
    grad_top = grad_out.reshape(rows_here, cols, cin)
    shards = lax.axis_size("dp") * row_count
    chunk = cin * wide // shards

    def spread(term):
        flat_term = (term / images).reshape(shards, 8, -1)
        return scatter_streams(flat_term, SCATTER_ORDERS, [512])

    def spread_still(term):
        return jnp.zeros((chunk,), jnp.float32)

    sent_top = passed_along(grad_top, "segment", 1)
    sent_mid = passed_along(grad_proj, "segment", 1)
    sent_top, sent_mid, grad_out = lax.optimization_barrier((sent_top, sent_mid, grad_out))

    def term_branch():
        return jnp.dot(
            grad_out.T, held.reshape(cells_here, wide), preferred_element_type=jnp.float32
        )

    def term_still():
        return jnp.zeros((cin, wide), jnp.float32)

    head_term = lax.cond(segment == 0, term_branch, term_still)
    head_share = lax.cond(segment == 0, spread, spread_still, head_term)
    head_share, sent_top, sent_mid, act = lax.optimization_barrier(
        (head_share, sent_top, sent_mid, act)
    )
    grad_part = jnp.sum(sent_mid.astype(jnp.float32) * act, axis=(0, 1))
    pool_total, grad_total = rows_sum((pool_part, grad_part))

    def gate_branch():
        gate, dpool = squeeze_gate(pool_total, grad_total, cells, reduce_w, expand_w)
        return ((sent_mid.astype(jnp.float32) * gate + dpool / cells) * silu_slope(dwo)).astype(
            jnp.bfloat16
        )

    def quiet_branch():
        return jnp.zeros((rows_here, cols, wide), jnp.bfloat16)

    grad_dw = lax.cond(segment == 1, gate_branch, quiet_branch)
    padded_grad = margin(grad_dw)

    def tail_branch():
        grad_e = depth_backward(padded_grad, taps, rows_here, cols)
        grad_pre = (
            (grad_e * silu_slope(held.astype(jnp.float32)))
            .astype(jnp.bfloat16)
            .reshape(cells_here, wide)
        )
        term = jnp.dot(
            image.reshape(cells_here, cin).T, grad_pre, preferred_element_type=jnp.float32
        )
        back = jnp.dot(grad_pre, weight.T, preferred_element_type=jnp.float32)
        grad_x = (sent_top.reshape(cells_here, cin).astype(jnp.float32) + back).astype(jnp.bfloat16)
        return (grad_x.reshape(rows_here, cols, cin), spread(term))

    def head_keep():
        return (grad_top, head_share)

    grad_here, share = lax.cond(segment == 1, tail_branch, head_keep)
    return (grad_here[None, None], share[None])


def solution(mesh):
    in_specs = (
        P("dp", "rows", None, None),
        P("segment", "dp", "rows", None, None),
        P("dp", "rows", None, None),
        P("dp", "rows", None, None),
        P("dp", "rows", None, None),
        P(),
        P("segment", ("dp", "rows")),
        P(),
        P(),
        P(),
    )
    out_specs = (P("segment", "dp", "rows", None, None), P("segment", ("dp", "rows")))
    return jax.shard_map(body, mesh=mesh, in_specs=in_specs, out_specs=out_specs, check_vma=False)
```

```python
import jax
import jax.numpy as jnp
from jax import lax
from jax.sharding import PartitionSpec as P


def extended_2(block, sides, width):
    for axis, dim in sides:
        count = lax.axis_size(axis)
        forward = [(i, i + 1) for i in range(count - 1)]
        backward = [(target, source) for source, target in forward]
        low = lax.ppermute(
            lax.slice_in_dim(block, block.shape[dim] - width, None, axis=dim), axis, forward
        )
        high = lax.ppermute(lax.slice_in_dim(block, 0, width, axis=dim), axis, backward)
        block = jnp.concatenate([low, block, high], axis=dim)
    return block


def passed_along(array, axis, by):
    length = lax.axis_size(axis)
    pairs = [(i, i + by) for i in range(length) if 0 <= i + by < length]
    return lax.ppermute(array, axis, pairs)


def flat_bits():
    rows_bits = lax.axis_size("rows").bit_length() - 1
    dp_bits = lax.axis_size("dp").bit_length() - 1
    return [("rows", k) for k in range(rows_bits)] + [("dp", k) for k in range(dp_bits)]


def swap_pairs(axis, j):
    return [(i, i ^ (1 << j)) for i in range(lax.axis_size(axis))]


def gather_chunks(piece, order):
    bits = flat_bits()
    buf = piece
    lead = []
    for axis, j in order:
        recv = lax.ppermute(buf, axis, swap_pairs(axis, j))
        high = (lax.axis_index(axis) >> j) & 1
        buf = jnp.stack([jnp.where(high == 0, buf, recv), jnp.where(high == 0, recv, buf)])
        lead.insert(0, bits.index((axis, j)))
    count = len(bits)
    perm = [lead.index(k) for k in reversed(range(count))] + [count, count + 1]
    return jnp.transpose(buf, perm).reshape((2**count,) + piece.shape)


def gather_streams(piece, orders, cuts):
    parts = jnp.split(piece, cuts, axis=-1)
    done = [gather_chunks(part, order) for part, order in zip(parts, orders)]
    return jnp.concatenate(done, axis=-1).reshape(-1)


def scatter_chunks(full, order, narrow=2):
    bits = flat_bits()
    count = len(bits)
    buf = full.reshape((2,) * count + full.shape[1:])
    live = list(reversed(range(count)))
    for step, (axis, j) in enumerate(order):
        at = live.index(bits.index((axis, j)))
        high = (lax.axis_index(axis) >> j) & 1
        mine = lax.dynamic_index_in_dim(buf, high, at, keepdims=False)
        other = lax.dynamic_index_in_dim(buf, 1 - high, at, keepdims=False)
        shape = other.shape
        if step < narrow:
            other = other.reshape(shape[:-3] + (-1, shape[-1])).astype(jnp.bfloat16)
        moved = lax.ppermute(other, axis, swap_pairs(axis, j))
        buf = mine + moved.astype(jnp.float32).reshape(shape)
        live.pop(at)
    return buf


def scatter_streams(full, orders, cuts):
    parts = jnp.split(full, cuts, axis=-1)
    done = [scatter_chunks(part, order) for part, order in zip(parts, orders)]
    return jnp.concatenate(done, axis=-1).reshape(-1)


def rows_sum(values):
    total = jnp.stack(values)
    for j in range(lax.axis_size("rows").bit_length() - 1):
        total = total + lax.ppermute(total, "rows", swap_pairs("rows", j))
    return tuple(total)


GATHER_ORDERS = (
    [("dp", 2), ("dp", 4), ("dp", 1), ("rows", 1), ("dp", 3), ("dp", 0), ("rows", 0)],
    [("dp", 4), ("rows", 1), ("dp", 2), ("dp", 1), ("rows", 0), ("dp", 3), ("dp", 0)],
)
SCATTER_ORDERS = tuple(order[::-1] for order in GATHER_ORDERS)


def up_two(v):
    return jnp.repeat(jnp.repeat(v, 2, axis=0), 2, axis=1)


def silu_slope(v):
    sig = jax.nn.sigmoid(v)
    return sig * (1.0 + v * (1.0 - sig))


def depth_forward(padded, taps, rows, cols):
    total = jnp.zeros((rows, cols, taps.shape[1]), jnp.float32)
    for p in range(5):
        for q in range(5):
            total = total + taps[5 * p + q] * padded[p : p + rows, q : q + cols].astype(jnp.float32)
    return total


def depth_backward(padded, taps, rows, cols):
    total = jnp.zeros((rows, cols, taps.shape[1]), jnp.float32)
    for p in range(5):
        for q in range(5):
            total = total + taps[5 * p + q] * padded[
                4 - p : 4 - p + rows, 4 - q : 4 - q + cols
            ].astype(jnp.float32)
    return total


def margin(values):
    extended = extended_2(values, (("rows", 0),), 2)
    return jnp.pad(extended, ((0, 0), (2, 2), (0, 0)))


def squeeze_gate(pool_total, grad_total, cells, reduce_w, expand_w):
    pooled = pool_total / cells
    z1 = jnp.dot(pooled, reduce_w, precision=lax.Precision.HIGHEST)
    z2 = jnp.dot(jax.nn.silu(z1), expand_w, precision=lax.Precision.HIGHEST)
    gate = jax.nn.sigmoid(z2)
    dz2 = grad_total * gate * (1.0 - gate)
    dz1 = jnp.dot(dz2, expand_w.T, precision=lax.Precision.HIGHEST) * silu_slope(z1)
    dpool = jnp.dot(dz1, reduce_w.T, precision=lax.Precision.HIGHEST)
    return (gate, dpool)


def body(
    block_input,
    saved_maps,
    grad_p5,
    grad_p6,
    grad_p7,
    lateral,
    stacked,
    kernel,
    se_reduce,
    se_expand,
):
    rows_here = block_input.shape[1]
    cols = block_input.shape[2]
    cin = block_input.shape[3]
    wide = saved_maps.shape[-1]
    cells_here = rows_here * cols
    row_count = lax.axis_size("rows")
    cells = cells_here * row_count
    images = block_input.shape[0] * lax.axis_size("dp")
    flat = gather_streams(stacked[0].reshape(16, -1), GATHER_ORDERS, [254])
    weight = flat.reshape(cin, wide)
    segment = lax.axis_index("segment")
    held = saved_maps[0, 0]
    image = block_input[0]
    taps = kernel.astype(jnp.float32)
    reduce_w = se_reduce.astype(jnp.float32)
    expand_w = se_expand.astype(jnp.float32)

    def rise_branch():
        return jax.nn.silu(held.astype(jnp.float32)).astype(jnp.bfloat16)

    def rise_still():
        return jnp.zeros((rows_here, cols, wide), jnp.bfloat16)

    expanded = lax.cond(segment == 1, rise_branch, rise_still)
    padded_e = margin(expanded)

    def pool_branch():
        dwo = depth_forward(padded_e, taps, rows_here, cols)
        act = jax.nn.silu(dwo)
        return (dwo, act, jnp.sum(act, axis=(0, 1)))

    def still_branch():
        return (
            jnp.zeros((rows_here, cols, wide), jnp.float32),
            jnp.zeros((rows_here, cols, wide), jnp.float32),
            jnp.zeros((wide,), jnp.float32),
        )

    dwo, act, pool_part = lax.cond(segment == 1, pool_branch, still_branch)

    def lead_branch():
        inner = grad_p6[0].astype(jnp.float32) + up_two(grad_p7[0].astype(jnp.float32)) / 4.0
        g = (grad_p5[0].astype(jnp.float32) + up_two(inner) / 4.0).astype(jnp.bfloat16)
        return jnp.dot(
            g.reshape(cells_here, -1), lateral.T, preferred_element_type=jnp.float32
        ).astype(jnp.bfloat16)

    def lead_still():
        return jnp.zeros((cells_here, cin), jnp.bfloat16)

    grad_out = lax.cond(segment == 0, lead_branch, lead_still)

    def head_branch():
        return jnp.dot(grad_out, weight, preferred_element_type=jnp.float32).astype(jnp.bfloat16)

    def head_still():
        return jnp.zeros((cells_here, wide), jnp.bfloat16)

    grad_proj = lax.cond(segment == 0, head_branch, head_still).reshape(rows_here, cols, wide)
    grad_top = grad_out.reshape(rows_here, cols, cin)
    shards = lax.axis_size("dp") * row_count
    chunk = cin * wide // shards

    def spread(term):
        flat_term = (term / images).reshape(shards, 8, -1)
        return scatter_streams(flat_term, SCATTER_ORDERS, [512])

    def spread_still(term):
        return jnp.zeros((chunk,), jnp.float32)

    sent_top, sent_mid = passed_along((grad_top, grad_proj), "segment", 1)
    sent_top, sent_mid, grad_out = lax.optimization_barrier((sent_top, sent_mid, grad_out))

    def term_branch():
        return jnp.dot(
            grad_out.T, held.reshape(cells_here, wide), preferred_element_type=jnp.float32
        )

    def term_still():
        return jnp.zeros((cin, wide), jnp.float32)

    head_term = lax.cond(segment == 0, term_branch, term_still)
    head_share = lax.cond(segment == 0, spread, spread_still, head_term)
    head_share, sent_top, sent_mid, act = lax.optimization_barrier(
        (head_share, sent_top, sent_mid, act)
    )
    (pool_total,) = rows_sum((pool_part,))
    grad_part = jnp.sum(sent_mid.astype(jnp.float32) * act, axis=(0, 1))
    (grad_total,) = rows_sum((grad_part,))

    def gate_branch():
        gate, dpool = squeeze_gate(pool_total, grad_total, cells, reduce_w, expand_w)
        return ((sent_mid.astype(jnp.float32) * gate + dpool / cells) * silu_slope(dwo)).astype(
            jnp.bfloat16
        )

    def quiet_branch():
        return jnp.zeros((rows_here, cols, wide), jnp.bfloat16)

    grad_dw = lax.cond(segment == 1, gate_branch, quiet_branch)
    padded_grad = margin(grad_dw)

    def tail_branch():
        grad_e = depth_backward(padded_grad, taps, rows_here, cols)
        grad_pre = (
            (grad_e * silu_slope(held.astype(jnp.float32)))
            .astype(jnp.bfloat16)
            .reshape(cells_here, wide)
        )
        term = jnp.dot(
            image.reshape(cells_here, cin).T, grad_pre, preferred_element_type=jnp.float32
        )
        back = jnp.dot(grad_pre, weight.T, preferred_element_type=jnp.float32)
        grad_x = (sent_top.reshape(cells_here, cin).astype(jnp.float32) + back).astype(jnp.bfloat16)
        return (grad_x.reshape(rows_here, cols, cin), spread(term))

    def head_keep():
        return (grad_top, head_share)

    grad_here, share = lax.cond(segment == 1, tail_branch, head_keep)
    return (grad_here[None, None], share[None])


def solution(mesh):
    in_specs = (
        P("dp", "rows", None, None),
        P("segment", "dp", "rows", None, None),
        P("dp", "rows", None, None),
        P("dp", "rows", None, None),
        P("dp", "rows", None, None),
        P(),
        P("segment", ("dp", "rows")),
        P(),
        P(),
        P(),
    )
    out_specs = (P("segment", "dp", "rows", None, None), P("segment", ("dp", "rows")))
    return jax.shard_map(body, mesh=mesh, in_specs=in_specs, out_specs=out_specs, check_vma=False)
```

```python
import jax
import jax.numpy as jnp
from jax import lax
from jax.sharding import PartitionSpec as P


def extended_2(block, sides, width):
    for axis, dim in sides:
        count = lax.axis_size(axis)
        forward = [(i, i + 1) for i in range(count - 1)]
        backward = [(target, source) for source, target in forward]
        low = lax.ppermute(
            lax.slice_in_dim(block, block.shape[dim] - width, None, axis=dim), axis, forward
        )
        high = lax.ppermute(lax.slice_in_dim(block, 0, width, axis=dim), axis, backward)
        block = jnp.concatenate([low, block, high], axis=dim)
    return block


def passed_along(array, axis, by):
    length = lax.axis_size(axis)
    pairs = [(i, i + by) for i in range(length) if 0 <= i + by < length]
    return lax.ppermute(array, axis, pairs)


def flat_bits():
    rows_bits = lax.axis_size("rows").bit_length() - 1
    dp_bits = lax.axis_size("dp").bit_length() - 1
    return [("rows", k) for k in range(rows_bits)] + [("dp", k) for k in range(dp_bits)]


def swap_pairs(axis, j):
    return [(i, i ^ (1 << j)) for i in range(lax.axis_size(axis))]


def gather_chunks(piece, order):
    bits = flat_bits()
    buf = piece
    lead = []
    for axis, j in order:
        recv = lax.ppermute(buf, axis, swap_pairs(axis, j))
        high = (lax.axis_index(axis) >> j) & 1
        buf = jnp.stack([jnp.where(high == 0, buf, recv), jnp.where(high == 0, recv, buf)])
        lead.insert(0, bits.index((axis, j)))
    count = len(bits)
    perm = [lead.index(k) for k in reversed(range(count))] + [count, count + 1]
    return jnp.transpose(buf, perm).reshape((2**count,) + piece.shape)


def gather_streams(piece, orders, cuts):
    parts = jnp.split(piece, cuts, axis=-1)
    done = [gather_chunks(part, order) for part, order in zip(parts, orders)]
    return jnp.concatenate(done, axis=-1).reshape(-1)


def scatter_chunks(full, order, narrow=2):
    bits = flat_bits()
    count = len(bits)
    buf = full.reshape((2,) * count + full.shape[1:])
    live = list(reversed(range(count)))
    for step, (axis, j) in enumerate(order):
        at = live.index(bits.index((axis, j)))
        high = (lax.axis_index(axis) >> j) & 1
        mine = lax.dynamic_index_in_dim(buf, high, at, keepdims=False)
        other = lax.dynamic_index_in_dim(buf, 1 - high, at, keepdims=False)
        shape = other.shape
        if step < narrow:
            other = other.reshape(shape[:-3] + (-1, shape[-1])).astype(jnp.bfloat16)
        moved = lax.ppermute(other, axis, swap_pairs(axis, j))
        buf = mine + moved.astype(jnp.float32).reshape(shape)
        live.pop(at)
    return buf


def scatter_streams(full, orders):
    done = [scatter_chunks(full[:, k], order) for k, order in enumerate(orders)]
    return jnp.stack(done).reshape(-1)


def rows_sum(values):
    total = jnp.stack(values)
    for j in range(lax.axis_size("rows").bit_length() - 1):
        total = total + lax.ppermute(total, "rows", swap_pairs("rows", j))
    return tuple(total)


GATHER_ORDERS = (
    [("dp", 2), ("dp", 4), ("dp", 1), ("rows", 1), ("dp", 3), ("dp", 0), ("rows", 0)],
    [("dp", 4), ("rows", 1), ("dp", 2), ("dp", 1), ("rows", 0), ("dp", 3), ("dp", 0)],
)
SCATTER_ORDERS = tuple(order[::-1] for order in GATHER_ORDERS)


def up_two(v):
    return jnp.repeat(jnp.repeat(v, 2, axis=0), 2, axis=1)


def silu_slope(v):
    sig = jax.nn.sigmoid(v)
    return sig * (1.0 + v * (1.0 - sig))


def depth_forward(padded, taps, rows, cols):
    total = jnp.zeros((rows, cols, taps.shape[1]), jnp.float32)
    for p in range(5):
        for q in range(5):
            total = total + taps[5 * p + q] * padded[p : p + rows, q : q + cols].astype(jnp.float32)
    return total


def depth_backward(padded, taps, rows, cols):
    total = jnp.zeros((rows, cols, taps.shape[1]), jnp.float32)
    for p in range(5):
        for q in range(5):
            total = total + taps[5 * p + q] * padded[
                4 - p : 4 - p + rows, 4 - q : 4 - q + cols
            ].astype(jnp.float32)
    return total


def margin(values):
    extended = extended_2(values, (("rows", 0),), 2)
    return jnp.pad(extended, ((0, 0), (2, 2), (0, 0)))


def squeeze_gate(pool_total, grad_total, cells, reduce_w, expand_w):
    pooled = pool_total / cells
    z1 = jnp.dot(pooled, reduce_w, precision=lax.Precision.HIGHEST)
    z2 = jnp.dot(jax.nn.silu(z1), expand_w, precision=lax.Precision.HIGHEST)
    gate = jax.nn.sigmoid(z2)
    dz2 = grad_total * gate * (1.0 - gate)
    dz1 = jnp.dot(dz2, expand_w.T, precision=lax.Precision.HIGHEST) * silu_slope(z1)
    dpool = jnp.dot(dz1, reduce_w.T, precision=lax.Precision.HIGHEST)
    return (gate, dpool)


def body(
    block_input,
    saved_maps,
    grad_p5,
    grad_p6,
    grad_p7,
    lateral,
    stacked,
    kernel,
    se_reduce,
    se_expand,
):
    rows_here = block_input.shape[1]
    cols = block_input.shape[2]
    cin = block_input.shape[3]
    wide = saved_maps.shape[-1]
    cells_here = rows_here * cols
    row_count = lax.axis_size("rows")
    cells = cells_here * row_count
    images = block_input.shape[0] * lax.axis_size("dp")
    flat = gather_streams(stacked[0].reshape(16, -1), GATHER_ORDERS, [254])
    weight = flat.reshape(cin, wide)
    segment = lax.axis_index("segment")
    held = saved_maps[0, 0]
    image = block_input[0]
    taps = kernel.astype(jnp.float32)
    reduce_w = se_reduce.astype(jnp.float32)
    expand_w = se_expand.astype(jnp.float32)

    def rise_branch():
        return jax.nn.silu(held.astype(jnp.float32)).astype(jnp.bfloat16)

    def rise_still():
        return jnp.zeros((rows_here, cols, wide), jnp.bfloat16)

    expanded = lax.cond(segment == 1, rise_branch, rise_still)
    padded_e = margin(expanded)

    def pool_branch():
        dwo = depth_forward(padded_e, taps, rows_here, cols)
        act = jax.nn.silu(dwo)
        return (dwo, act, jnp.sum(act, axis=(0, 1)))

    def still_branch():
        return (
            jnp.zeros((rows_here, cols, wide), jnp.float32),
            jnp.zeros((rows_here, cols, wide), jnp.float32),
            jnp.zeros((wide,), jnp.float32),
        )

    dwo, act, pool_part = lax.cond(segment == 1, pool_branch, still_branch)

    def lead_branch():
        inner = grad_p6[0].astype(jnp.float32) + up_two(grad_p7[0].astype(jnp.float32)) / 4.0
        g = (grad_p5[0].astype(jnp.float32) + up_two(inner) / 4.0).astype(jnp.bfloat16)
        return jnp.dot(
            g.reshape(cells_here, -1), lateral.T, preferred_element_type=jnp.float32
        ).astype(jnp.bfloat16)

    def lead_still():
        return jnp.zeros((cells_here, cin), jnp.bfloat16)

    grad_out = lax.cond(segment == 0, lead_branch, lead_still)

    def head_branch():
        return jnp.dot(grad_out, weight, preferred_element_type=jnp.float32).astype(jnp.bfloat16)

    def head_still():
        return jnp.zeros((cells_here, wide), jnp.bfloat16)

    grad_proj = lax.cond(segment == 0, head_branch, head_still).reshape(rows_here, cols, wide)
    grad_top = grad_out.reshape(rows_here, cols, cin)
    shards = lax.axis_size("dp") * row_count
    chunk = cin * wide // shards

    def spread(term):
        flat_term = (term / images).reshape(shards, len(SCATTER_ORDERS), 8, -1)
        return scatter_streams(flat_term, SCATTER_ORDERS)

    def spread_still(term):
        return jnp.zeros((chunk,), jnp.float32)

    sent_top, sent_mid = passed_along((grad_top, grad_proj), "segment", 1)
    sent_top, sent_mid, grad_out = lax.optimization_barrier((sent_top, sent_mid, grad_out))

    def term_branch():
        return jnp.dot(
            grad_out.T, held.reshape(cells_here, wide), preferred_element_type=jnp.float32
        )

    def term_still():
        return jnp.zeros((cin, wide), jnp.float32)

    head_term = lax.cond(segment == 0, term_branch, term_still)
    head_share = lax.cond(segment == 0, spread, spread_still, head_term)
    head_share, sent_top, sent_mid, act = lax.optimization_barrier(
        (head_share, sent_top, sent_mid, act)
    )
    (pool_total,) = rows_sum((pool_part,))
    grad_part = jnp.sum(sent_mid.astype(jnp.float32) * act, axis=(0, 1))
    (grad_total,) = rows_sum((grad_part,))

    def gate_branch():
        gate, dpool = squeeze_gate(pool_total, grad_total, cells, reduce_w, expand_w)
        return ((sent_mid.astype(jnp.float32) * gate + dpool / cells) * silu_slope(dwo)).astype(
            jnp.bfloat16
        )

    def quiet_branch():
        return jnp.zeros((rows_here, cols, wide), jnp.bfloat16)

    grad_dw = lax.cond(segment == 1, gate_branch, quiet_branch)
    padded_grad = margin(grad_dw)

    def tail_branch():
        grad_e = depth_backward(padded_grad, taps, rows_here, cols)
        grad_pre = (
            (grad_e * silu_slope(held.astype(jnp.float32)))
            .astype(jnp.bfloat16)
            .reshape(cells_here, wide)
        )
        term = jnp.dot(
            image.reshape(cells_here, cin).T, grad_pre, preferred_element_type=jnp.float32
        )
        back = jnp.dot(grad_pre, weight.T, preferred_element_type=jnp.float32)
        grad_x = (sent_top.reshape(cells_here, cin).astype(jnp.float32) + back).astype(jnp.bfloat16)
        return (grad_x.reshape(rows_here, cols, cin), spread(term))

    def head_keep():
        return (grad_top, head_share)

    grad_here, share = lax.cond(segment == 1, tail_branch, head_keep)
    return (grad_here[None, None], share[None])


def solution(mesh):
    in_specs = (
        P("dp", "rows", None, None),
        P("segment", "dp", "rows", None, None),
        P("dp", "rows", None, None),
        P("dp", "rows", None, None),
        P("dp", "rows", None, None),
        P(),
        P("segment", ("dp", "rows")),
        P(),
        P(),
        P(),
    )
    out_specs = (P("segment", "dp", "rows", None, None), P("segment", ("dp", "rows")))
    return jax.shard_map(body, mesh=mesh, in_specs=in_specs, out_specs=out_specs, check_vma=False)
```

```python
import jax
import jax.numpy as jnp
from jax import lax
from jax.sharding import PartitionSpec as P


def extended_2(block, sides, width):
    for axis, dim in sides:
        count = lax.axis_size(axis)
        forward = [(i, i + 1) for i in range(count - 1)]
        backward = [(target, source) for source, target in forward]
        low = lax.ppermute(
            lax.slice_in_dim(block, block.shape[dim] - width, None, axis=dim), axis, forward
        )
        high = lax.ppermute(lax.slice_in_dim(block, 0, width, axis=dim), axis, backward)
        block = jnp.concatenate([low, block, high], axis=dim)
    return block


def passed_along(array, axis, by):
    length = lax.axis_size(axis)
    pairs = [(i, i + by) for i in range(length) if 0 <= i + by < length]
    return lax.ppermute(array, axis, pairs)


def flat_bits():
    rows_bits = lax.axis_size("rows").bit_length() - 1
    dp_bits = lax.axis_size("dp").bit_length() - 1
    return [("rows", k) for k in range(rows_bits)] + [("dp", k) for k in range(dp_bits)]


def swap_pairs(axis, j):
    return [(i, i ^ (1 << j)) for i in range(lax.axis_size(axis))]


def gather_chunks(piece, order):
    bits = flat_bits()
    buf = piece
    lead = []
    for axis, j in order:
        recv = lax.ppermute(buf, axis, swap_pairs(axis, j))
        high = (lax.axis_index(axis) >> j) & 1
        buf = jnp.stack([jnp.where(high == 0, buf, recv), jnp.where(high == 0, recv, buf)])
        lead.insert(0, bits.index((axis, j)))
    count = len(bits)
    perm = [lead.index(k) for k in reversed(range(count))] + [count, count + 1]
    return jnp.transpose(buf, perm).reshape((2**count,) + piece.shape)


def gather_streams(piece, orders, cuts):
    parts = jnp.split(piece, cuts, axis=-1)
    done = [gather_chunks(part, order) for part, order in zip(parts, orders)]
    return jnp.concatenate(done, axis=-1).reshape(-1)


def scatter_chunks(full, order, narrow=3):
    bits = flat_bits()
    count = len(bits)
    buf = full.reshape((2,) * count + full.shape[1:])
    live = list(reversed(range(count)))
    for step, (axis, j) in enumerate(order):
        at = live.index(bits.index((axis, j)))
        high = (lax.axis_index(axis) >> j) & 1
        mine = lax.dynamic_index_in_dim(buf, high, at, keepdims=False)
        other = lax.dynamic_index_in_dim(buf, 1 - high, at, keepdims=False)
        shape = other.shape
        if step < narrow:
            other = other.reshape(shape[:-3] + (-1, shape[-1])).astype(jnp.bfloat16)
        moved = lax.ppermute(other, axis, swap_pairs(axis, j))
        buf = mine + moved.astype(jnp.float32).reshape(shape)
        live.pop(at)
    return buf


def scatter_streams(full, orders, cuts):
    parts = jnp.split(full, cuts, axis=-1)
    done = [scatter_chunks(part, order) for part, order in zip(parts, orders)]
    return jnp.concatenate(done, axis=-1).reshape(-1)


def rows_sum(values):
    total = jnp.stack(values)
    for j in range(lax.axis_size("rows").bit_length() - 1):
        total = total + lax.ppermute(total, "rows", swap_pairs("rows", j))
    return tuple(total)


GATHER_ORDERS = (
    [("dp", 2), ("dp", 4), ("dp", 1), ("rows", 1), ("dp", 3), ("dp", 0), ("rows", 0)],
    [("dp", 4), ("rows", 1), ("dp", 2), ("dp", 1), ("rows", 0), ("dp", 3), ("dp", 0)],
)
SCATTER_ORDERS = tuple(order[::-1] for order in GATHER_ORDERS)


def up_two(v):
    return jnp.repeat(jnp.repeat(v, 2, axis=0), 2, axis=1)


def silu_slope(v):
    sig = jax.nn.sigmoid(v)
    return sig * (1.0 + v * (1.0 - sig))


def depth_forward(padded, taps, rows, cols):
    total = jnp.zeros((rows, cols, taps.shape[1]), jnp.float32)
    for p in range(5):
        for q in range(5):
            total = total + taps[5 * p + q] * padded[p : p + rows, q : q + cols].astype(jnp.float32)
    return total


def depth_backward(padded, taps, rows, cols):
    total = jnp.zeros((rows, cols, taps.shape[1]), jnp.float32)
    for p in range(5):
        for q in range(5):
            total = total + taps[5 * p + q] * padded[
                4 - p : 4 - p + rows, 4 - q : 4 - q + cols
            ].astype(jnp.float32)
    return total


def margin(values):
    extended = extended_2(values, (("rows", 0),), 2)
    return jnp.pad(extended, ((0, 0), (2, 2), (0, 0)))


def squeeze_gate(pool_total, grad_total, cells, reduce_w, expand_w):
    pooled = pool_total / cells
    z1 = jnp.dot(pooled, reduce_w, precision=lax.Precision.HIGHEST)
    z2 = jnp.dot(jax.nn.silu(z1), expand_w, precision=lax.Precision.HIGHEST)
    gate = jax.nn.sigmoid(z2)
    dz2 = grad_total * gate * (1.0 - gate)
    dz1 = jnp.dot(dz2, expand_w.T, precision=lax.Precision.HIGHEST) * silu_slope(z1)
    dpool = jnp.dot(dz1, reduce_w.T, precision=lax.Precision.HIGHEST)
    return (gate, dpool)


def body(
    block_input,
    saved_maps,
    grad_p5,
    grad_p6,
    grad_p7,
    lateral,
    stacked,
    kernel,
    se_reduce,
    se_expand,
):
    rows_here = block_input.shape[1]
    cols = block_input.shape[2]
    cin = block_input.shape[3]
    wide = saved_maps.shape[-1]
    cells_here = rows_here * cols
    row_count = lax.axis_size("rows")
    cells = cells_here * row_count
    images = block_input.shape[0] * lax.axis_size("dp")
    flat = gather_streams(stacked[0].reshape(16, -1), GATHER_ORDERS, [254])
    weight = flat.reshape(cin, wide)
    segment = lax.axis_index("segment")
    held = saved_maps[0, 0]
    image = block_input[0]
    taps = kernel.astype(jnp.float32)
    reduce_w = se_reduce.astype(jnp.float32)
    expand_w = se_expand.astype(jnp.float32)

    def rise_branch():
        return jax.nn.silu(held.astype(jnp.float32)).astype(jnp.bfloat16)

    def rise_still():
        return jnp.zeros((rows_here, cols, wide), jnp.bfloat16)

    expanded = lax.cond(segment == 1, rise_branch, rise_still)
    padded_e = margin(expanded)

    def pool_branch():
        dwo = depth_forward(padded_e, taps, rows_here, cols)
        act = jax.nn.silu(dwo)
        return (dwo, act, jnp.sum(act, axis=(0, 1)))

    def still_branch():
        return (
            jnp.zeros((rows_here, cols, wide), jnp.float32),
            jnp.zeros((rows_here, cols, wide), jnp.float32),
            jnp.zeros((wide,), jnp.float32),
        )

    dwo, act, pool_part = lax.cond(segment == 1, pool_branch, still_branch)

    def lead_branch():
        inner = grad_p6[0].astype(jnp.float32) + up_two(grad_p7[0].astype(jnp.float32)) / 4.0
        g = (grad_p5[0].astype(jnp.float32) + up_two(inner) / 4.0).astype(jnp.bfloat16)
        return jnp.dot(
            g.reshape(cells_here, -1), lateral.T, preferred_element_type=jnp.float32
        ).astype(jnp.bfloat16)

    def lead_still():
        return jnp.zeros((cells_here, cin), jnp.bfloat16)

    grad_out = lax.cond(segment == 0, lead_branch, lead_still)

    def head_branch():
        return jnp.dot(grad_out, weight, preferred_element_type=jnp.float32).astype(jnp.bfloat16)

    def head_still():
        return jnp.zeros((cells_here, wide), jnp.bfloat16)

    grad_proj = lax.cond(segment == 0, head_branch, head_still).reshape(rows_here, cols, wide)
    grad_top = grad_out.reshape(rows_here, cols, cin)
    shards = lax.axis_size("dp") * row_count
    chunk = cin * wide // shards

    def spread(term):
        flat_term = (term / images).reshape(shards, 8, -1)
        return scatter_streams(flat_term, SCATTER_ORDERS, [512])

    def spread_still(term):
        return jnp.zeros((chunk,), jnp.float32)

    sent_top, sent_mid = passed_along((grad_top, grad_proj), "segment", 1)
    sent_top, sent_mid, grad_out = lax.optimization_barrier((sent_top, sent_mid, grad_out))

    def term_branch():
        return jnp.dot(
            grad_out.T, held.reshape(cells_here, wide), preferred_element_type=jnp.float32
        )

    def term_still():
        return jnp.zeros((cin, wide), jnp.float32)

    head_term = lax.cond(segment == 0, term_branch, term_still)
    head_share = lax.cond(segment == 0, spread, spread_still, head_term)
    head_share, sent_top, sent_mid, act = lax.optimization_barrier(
        (head_share, sent_top, sent_mid, act)
    )
    (pool_total,) = rows_sum((pool_part,))
    grad_part = jnp.sum(sent_mid.astype(jnp.float32) * act, axis=(0, 1))
    (grad_total,) = rows_sum((grad_part,))

    def gate_branch():
        gate, dpool = squeeze_gate(pool_total, grad_total, cells, reduce_w, expand_w)
        return ((sent_mid.astype(jnp.float32) * gate + dpool / cells) * silu_slope(dwo)).astype(
            jnp.bfloat16
        )

    def quiet_branch():
        return jnp.zeros((rows_here, cols, wide), jnp.bfloat16)

    grad_dw = lax.cond(segment == 1, gate_branch, quiet_branch)
    padded_grad = margin(grad_dw)

    def tail_branch():
        grad_e = depth_backward(padded_grad, taps, rows_here, cols)
        grad_pre = (
            (grad_e * silu_slope(held.astype(jnp.float32)))
            .astype(jnp.bfloat16)
            .reshape(cells_here, wide)
        )
        term = jnp.dot(
            image.reshape(cells_here, cin).T, grad_pre, preferred_element_type=jnp.float32
        )
        back = jnp.dot(grad_pre, weight.T, preferred_element_type=jnp.float32)
        grad_x = (sent_top.reshape(cells_here, cin).astype(jnp.float32) + back).astype(jnp.bfloat16)
        return (grad_x.reshape(rows_here, cols, cin), spread(term))

    def head_keep():
        return (grad_top, head_share)

    grad_here, share = lax.cond(segment == 1, tail_branch, head_keep)
    return (grad_here[None, None], share[None])


def solution(mesh):
    in_specs = (
        P("dp", "rows", None, None),
        P("segment", "dp", "rows", None, None),
        P("dp", "rows", None, None),
        P("dp", "rows", None, None),
        P("dp", "rows", None, None),
        P(),
        P("segment", ("dp", "rows")),
        P(),
        P(),
        P(),
    )
    out_specs = (P("segment", "dp", "rows", None, None), P("segment", ("dp", "rows")))
    return jax.shard_map(body, mesh=mesh, in_specs=in_specs, out_specs=out_specs, check_vma=False)
```
